32 devices in a mesh: ctx: 16 (over z, x, core), hg: 2 (over y).
Axes of the slice: x: 2, y: 2, z: 4, core: 2. Of those that a mesh axis runs over, the one named last changes fastest.
Arguments:
- queries: bfloat16 [4096, 2048], P(('ctx', 'hg')), may hold values from -6 to 6
- keys: bfloat16 [4096, 2048], P(('ctx', 'hg')), may hold values from -6 to 6
- values: bfloat16 [4096, 2048], P(('ctx', 'hg')), may hold values from -6 to 6
- reflect_ids: int32 [4096, 16], P('ctx', 'hg'), may hold values from 0 to 1023
- reflect_bank: bfloat16 [1024, 2048], P(None, 'hg'), may hold values from -6 to 6
- out_weight: bfloat16 [2048, 4096], P('hg'), may hold values from -0.125 to 0.125
Outputs:
- mixed: bfloat16 [4096, 4096], P(('ctx', 'hg'))
The draws below stay inside these ranges and needn't reach their ends.
All inputs are finite; a program needn't handle non-finite values.
Results may differ from the reference program's by a relative error of at most 0.013.
The reference program's roundings to bfloat16 on the way (of `weights` and `attn`) count: a program that leaves them out, or rounds other values in their place, can miss the bound.
Values may be sent and summed in bfloat16 or wider, within the bound.
No kernel may reach another device: no remote copies, remote signals or barrier semaphores. Data moves between devices by JAX's collectives and lax.ppermute only.
A program may use at most 192 MiB of HBM per device.

```python
import math
import jax
import jax.numpy as jnp
from jax import lax

D = 4096
HEADS = 16
HDIM = 128
BANK = 1024
TOKENS = 4096


def drawn_rows(key, salt):
    width = HEADS * HDIM
    sub = jax.random.fold_in(key, salt)
    return jnp.clip(1.6 * jax.random.normal(sub, (TOKENS, width), jnp.float32), -5.5, 5.5)


def draw_queries(key, part):
    result = drawn_rows(key, 7)
    return result.astype(jnp.bfloat16)


def draw_keys(key, part):
    result = drawn_rows(key, 8)
    return result.astype(jnp.bfloat16)


def with_ends(values, rng, smallest, high):
    index_at = [jax.random.randint(jax.random.fold_in(rng, axis), (), 0, length) for axis, length in enumerate(values.shape)]
    widest = values.shape.index(max(values.shape))
    next_to = index_at[:widest] + [(index_at[widest] + 1) % values.shape[widest]] + index_at[widest + 1:]
    return values.at[tuple(index_at)].set(smallest).at[tuple(next_to)].set(high)


def level_of(stream_key, shape, pieces, smallest, largest):
    factor_of = 1.0
    for dim, shards_of in pieces:
        draws = jax.random.uniform(jax.random.fold_in(jax.random.fold_in(stream_key, 6), dim), (shards_of,), jnp.float32, smallest / len(pieces), largest / len(pieces))
        factor_of = factor_of * jnp.repeat(jnp.exp(draws), shape[dim] // shards_of).reshape((-1,) + (1,) * (len(shape) - 1 - dim))
    return factor_of


def gaussian(stream_key, shape, deviation, bound, pieces=(), kind=jnp.bfloat16):
    values = jax.random.normal(stream_key, shape, jnp.float32) * deviation
    if len(pieces) > 0:
        values = level_of(stream_key, shape, pieces, -0.22, 0.18) * values
    return jnp.clip(values, min=-bound, max=bound).astype(kind)


def setup_inputs(seed: int = 0) -> dict:
    key_list = jax.random.split(jax.random.key(seed), 7)
    queries = draw_queries(jax.random.fold_in(key_list[6], 71), 0)
    keys = draw_keys(jax.random.fold_in(key_list[6], 71), 0)
    values = gaussian(key_list[2], (TOKENS, HEADS * HDIM), 1.0, 6.0, ((0, 32),))
    reflect_ids = with_ends(jax.random.randint(key_list[3], (TOKENS, HEADS), 0, BANK), jax.random.fold_in(key_list[3], 1), 0, BANK - 1).astype(jnp.int32)
    reflect_bank = gaussian(key_list[4], (BANK, HEADS * HDIM), 1.0, 6.0, ((1, 2),))
    out_weight = gaussian(key_list[5], (HEADS * HDIM, D), (HEADS * HDIM) ** -0.5, 0.125, ((0, 2),))
    return {"queries": queries, "keys": keys, "values": values, "reflect_ids": reflect_ids, "reflect_bank": reflect_bank, "out_weight": out_weight}


def reference(queries, keys, values, reflect_ids, reflect_bank, out_weight):
    hp = lax.Precision.HIGHEST
    table = reflect_bank.reshape(BANK, HEADS, HDIM)
    chosen = table[reflect_ids, jnp.arange(HEADS)[None, :]].astype(jnp.float32)
    vectors = chosen * lax.rsqrt(lax.optimization_barrier(jnp.sum(chosen * chosen, axis=-1, keepdims=True)) + 1e-06)
    q_rows = queries.astype(jnp.float32).reshape(TOKENS, HEADS, HDIM)
    k_rows = keys.astype(jnp.float32).reshape(TOKENS, HEADS, HDIM)

    def advance(frame, item):
        unit, q_one, k_one = item
        moved = jnp.einsum('hde,he->hd', frame, unit, precision=hp)
        frame = frame - 2.0 * moved[:, :, None] * unit[:, None, :]
        q_new = jnp.einsum('hde,he->hd', frame, q_one, precision=hp)
        k_new = jnp.einsum('hde,he->hd', frame, k_one, precision=hp)
        return (frame, (q_new, k_new))
    start_frame = jnp.broadcast_to(jnp.eye(HDIM, dtype=jnp.float32), (HEADS, HDIM, HDIM))
    _, (q_glob, k_glob) = lax.scan(advance, start_frame, (vectors, q_rows, k_rows))
    q_heads = q_glob.astype(jnp.bfloat16).transpose(1, 0, 2)
    k_heads = k_glob.astype(jnp.bfloat16).transpose(1, 0, 2)
    v_heads = values.reshape(TOKENS, HEADS, HDIM).transpose(1, 0, 2)
    qblock = math.gcd(TOKENS, 512)
    nqblocks = TOKENS // qblock
    scale = 1.0 / math.sqrt(HDIM)
    key_pos = jnp.arange(TOKENS, dtype=jnp.int32)

    def one_head(operands):
        q_head, k_head, v_head = operands

        def one_block(index):
            first = (index * qblock).astype(jnp.int32)
            q_part = lax.dynamic_slice_in_dim(q_head, first, qblock, 0)
            scores = jnp.dot(q_part, k_head.T, preferred_element_type=jnp.float32) * scale
            q_pos = first + jnp.arange(qblock, dtype=jnp.int32)
            allowed = key_pos[None, :] <= q_pos[:, None]
            scores = jnp.where(allowed, scores, -jnp.inf)
            rowmax = lax.optimization_barrier(jnp.max(scores, axis=-1, keepdims=True))
            expd = jnp.where(allowed, jnp.exp(scores - rowmax), 0.0)
            total = lax.optimization_barrier(jnp.sum(expd, axis=-1, keepdims=True))
            weights = expd.astype(jnp.bfloat16)
            numer = jnp.dot(weights, v_head, preferred_element_type=jnp.float32)
            return (numer / total).astype(jnp.bfloat16)
        parts = lax.map(one_block, jnp.arange(nqblocks, dtype=jnp.int32))
        return parts.reshape(TOKENS, HDIM)
    attn_heads = lax.map(one_head, (q_heads, k_heads, v_heads))
    attn = attn_heads.transpose(1, 0, 2).reshape(TOKENS, HEADS * HDIM)
    return jnp.dot(attn, out_weight, preferred_element_type=jnp.float32).astype(jnp.bfloat16)
```

```python
import math

import jax
import jax.numpy as jnp
from jax import lax
from jax.experimental import pallas as pl
from jax.experimental.pallas import tpu as pltpu
from jax.sharding import PartitionSpec as P

HDIM = 128
BLK = 32
HP = lax.Precision.HIGHEST


def mm(a, b):
    return jnp.einsum("...ij,...jk->...ik", a, b, precision=HP)


def invert_unit_upper(strict):
    eye_blk = jnp.eye(strict.shape[-1], dtype=jnp.float32)
    result = eye_blk - strict
    power = strict
    steps = strict.shape[-1].bit_length()
    for level in range(steps):
        power = mm(power, power)
        result = mm(result, eye_blk + power)
    return result


def exclusive_blocks(mats):
    heads, n, d, _ = mats.shape
    eye = jnp.broadcast_to(jnp.eye(d, dtype=jnp.float32), (heads, 1, d, d))
    acc = jnp.concatenate([eye, mats[:, :-1]], axis=1)
    shift = 1
    while shift < n:
        earlier = jnp.concatenate(
            [jnp.broadcast_to(eye, (heads, shift, d, d)), acc[:, : n - shift]], axis=1
        )
        acc = mm(earlier, acc)
        shift *= 2
    return acc, mm(acc[:, -1], mats[:, -1])


def exclusive_shards(mat, axis):
    length, here = lax.axis_size(axis), lax.axis_index(axis)
    eye = jnp.broadcast_to(jnp.eye(mat.shape[-1], dtype=jnp.float32), mat.shape)
    if length == 1:
        return eye
    acc = lax.ppermute(mat, axis, [(i, i + 1) for i in range(length - 1)])
    acc = jnp.where(here >= 1, acc, eye)
    shift = 1
    while shift < length:
        earlier = lax.ppermute(acc, axis, [(i, i + shift) for i in range(length - shift)])
        acc = jnp.where(here >= shift, mm(earlier, acc), acc)
        shift *= 2
    return acc


def flash_attend(q_glob, k_all, v_all, shard, heads):
    rows, width = q_glob.shape
    nk = k_all.shape[0] // rows
    scale = 1.0 / math.sqrt(HDIM)

    def kernel(c_ref, q_ref, k_ref, v_ref, o_ref, m_sc, l_sc, acc_sc):
        j = pl.program_id(0)
        c = c_ref[0]

        @pl.when(j == 0)
        def _():
            m_sc[...] = jnp.full(m_sc.shape, -1e30, jnp.float32)
            l_sc[...] = jnp.zeros(l_sc.shape, jnp.float32)
            acc_sc[...] = jnp.zeros(acc_sc.shape, jnp.float32)

        def step(masked):
            for hh in range(heads):
                sl = slice(hh * HDIM, (hh + 1) * HDIM)
                qh = q_ref[:, sl]
                kh = k_ref[:, sl]
                vh = v_ref[:, sl]
                s = (
                    lax.dot_general(
                        qh, kh, (((1,), (1,)), ((), ())), preferred_element_type=jnp.float32
                    )
                    * scale
                )
                if masked:
                    row = lax.broadcasted_iota(jnp.int32, s.shape, 0)
                    col = lax.broadcasted_iota(jnp.int32, s.shape, 1)
                    allowed = col <= row
                    s = jnp.where(allowed, s, -1e30)
                m_prev = m_sc[hh]
                m_new = jnp.maximum(m_prev, jnp.max(s, axis=1, keepdims=True))
                p = jnp.exp(s - m_new)
                if masked:
                    p = jnp.where(allowed, p, 0.0)
                fade = jnp.exp(m_prev - m_new)
                l_sc[hh] = l_sc[hh] * fade + jnp.sum(p, axis=1, keepdims=True)
                acc_sc[hh] = acc_sc[hh] * fade + jnp.dot(
                    p.astype(jnp.bfloat16), vh, preferred_element_type=jnp.float32
                )
                m_sc[hh] = m_new

        @pl.when(j < c)
        def _():
            step(False)

        @pl.when(j == c)
        def _():
            step(True)

        @pl.when(j == nk - 1)
        def _():
            for hh in range(heads):
                sl = slice(hh * HDIM, (hh + 1) * HDIM)
                o_ref[:, sl] = (acc_sc[hh] / l_sc[hh]).astype(o_ref.dtype)

    grid_spec = pltpu.PrefetchScalarGridSpec(
        num_scalar_prefetch=1,
        grid=(nk,),
        in_specs=[
            pl.BlockSpec((rows, width), lambda j, c: (0, 0)),
            pl.BlockSpec((rows, width), lambda j, c: (jnp.minimum(j, c[0]), 0)),
            pl.BlockSpec((rows, width), lambda j, c: (jnp.minimum(j, c[0]), 0)),
        ],
        out_specs=pl.BlockSpec((rows, width), lambda j, c: (0, 0)),
        scratch_shapes=[
            pltpu.VMEM((heads, rows, 1), jnp.float32),
            pltpu.VMEM((heads, rows, 1), jnp.float32),
            pltpu.VMEM((heads, rows, HDIM), jnp.float32),
        ],
    )
    return pl.pallas_call(
        kernel,
        grid_spec=grid_spec,
        out_shape=jax.ShapeDtypeStruct((rows, width), jnp.bfloat16),
        compiler_params=pltpu.CompilerParams(dimension_semantics=("arbitrary",)),
    )(jnp.reshape(shard, (1,)).astype(jnp.int32), q_glob, k_all, v_all)


def local(queries, keys, values, reflect_ids, reflect_bank, out_weight):
    groups = lax.axis_size("hg")
    heads = reflect_ids.shape[1]
    width = heads * HDIM
    stacked = jnp.stack([queries, keys, values], axis=1).reshape(
        queries.shape[0], 3, groups, width
    )
    swapped = lax.all_to_all(stacked, "hg", split_axis=2, concat_axis=0, tiled=True)
    rows = swapped.shape[0]
    q_local = swapped[:, 0, 0]
    k_local = swapped[:, 1, 0]
    v_local = swapped[:, 2, 0]
    v_all = lax.all_gather(v_local, "ctx", axis=0, tiled=True)

    nblocks = rows // BLK
    bank = reflect_bank.shape[0]
    table = reflect_bank.reshape(bank, heads, HDIM).transpose(1, 0, 2)
    onehot = (
        reflect_ids.T[:, :, None] == lax.broadcasted_iota(jnp.int32, (1, 1, bank), 2)
    ).astype(reflect_bank.dtype)
    chosen = jnp.einsum(
        "htb,hbd->htd", onehot, table, preferred_element_type=jnp.float32
    )
    vectors = chosen * lax.rsqrt(jnp.sum(chosen * chosen, axis=-1, keepdims=True) + 1e-06)
    blocks = vectors.reshape(heads, nblocks, BLK, HDIM)
    gram = jnp.einsum("hnkd,hnjd->hnkj", blocks, blocks, precision=HP)
    coupling = 2.0 * jnp.triu(gram, 1)
    tri_factor = 2.0 * invert_unit_upper(coupling)
    spread = jnp.einsum("hnkj,hnje->hnke", tri_factor, blocks, precision=HP)
    eye_d = jnp.eye(HDIM, dtype=jnp.float32)
    block_mats = eye_d - jnp.einsum("hnkd,hnke->hnde", blocks, spread, precision=HP)
    lower_mask = jnp.tril(jnp.ones((BLK, BLK), dtype=jnp.bool_))

    inner_prefix, shard_prod = exclusive_blocks(block_mats)
    earlier_prod = exclusive_shards(shard_prod, "ctx")

    def in_shard(matrix):
        split = matrix.astype(jnp.float32).reshape(nblocks, BLK, heads, HDIM).transpose(2, 0, 1, 3)
        proj = jnp.einsum("hnid,hnkd->hnik", split, blocks, precision=HP)
        proj = jnp.where(lower_mask, proj, 0.0)
        coef = jnp.einsum("hnik,hnrk->hnir", proj, tri_factor, precision=HP)
        inblock = split - jnp.einsum("hnir,hnrd->hnid", coef, blocks, precision=HP)
        moved = jnp.einsum("hnid,hned->hnie", inblock, inner_prefix, precision=HP)
        return moved.reshape(heads, rows, HDIM)

    def to_global(moved):
        full = jnp.einsum("hie,hfe->hif", moved, earlier_prod, precision=HP)
        return full.transpose(1, 0, 2).reshape(rows, width).astype(jnp.bfloat16)

    k_glob = to_global(in_shard(k_local))
    k_all = lax.all_gather(k_glob, "ctx", axis=0, tiled=True)
    q_glob = to_global(in_shard(q_local))

    attn = flash_attend(q_glob, k_all, v_all, lax.axis_index("ctx"), heads)
    return lax.psum_scatter(
        jnp.dot(attn, out_weight, preferred_element_type=jnp.float32).astype(jnp.bfloat16),
        "hg",
        scatter_dimension=0,
        tiled=True,
    )


def solution(mesh):
    placed = (
        P(("ctx", "hg"), None),
        P(("ctx", "hg"), None),
        P(("ctx", "hg"), None),
        P("ctx", "hg"),
        P(None, "hg"),
        P("hg", None),
    )
    return jax.shard_map(
        local, mesh=mesh, in_specs=placed, out_specs=P(("ctx", "hg"), None), check_vma=False
    )
```

```python
import math

import jax
import jax.numpy as jnp
from jax import lax
from jax.experimental import pallas as pl
from jax.experimental.pallas import tpu as pltpu
from jax.sharding import PartitionSpec as P

HDIM = 128
BLK = 32
HP = lax.Precision.HIGHEST


def mm(a, b):
    return jnp.einsum("...ij,...jk->...ik", a, b, precision=HP)


def invert_unit_upper(strict):
    eye_blk = jnp.eye(strict.shape[-1], dtype=jnp.float32)
    result = eye_blk - strict
    power = strict
    steps = strict.shape[-1].bit_length()
    for level in range(steps):
        power = mm(power, power)
        result = mm(result, eye_blk + power)
    return result


def exclusive_blocks(mats):
    heads, n, d, _ = mats.shape
    eye = jnp.broadcast_to(jnp.eye(d, dtype=jnp.float32), (heads, 1, d, d))
    acc = jnp.concatenate([eye, mats[:, :-1]], axis=1)
    shift = 1
    while shift < n:
        earlier = jnp.concatenate(
            [jnp.broadcast_to(eye, (heads, shift, d, d)), acc[:, : n - shift]], axis=1
        )
        acc = mm(earlier, acc)
        shift *= 2
    return acc, mm(acc[:, -1], mats[:, -1])


SWAP = [(0, 1), (1, 0)]


def chip_gather(x):
    mine = lax.all_gather(x, "chip", axis=0, tiled=False)
    return mine, lax.ppermute(mine, "core", SWAP)


def exclusive_shards(mat):
    core = lax.axis_index("core")
    chip = lax.axis_index("chip")
    nchip = lax.axis_size("chip")
    eye = jnp.broadcast_to(jnp.eye(mat.shape[-1], dtype=jnp.float32), mat.shape)
    partner = lax.ppermute(mat, "core", SWAP)
    pair = jnp.where(core == 0, mm(mat, partner), mm(partner, mat))
    pairs = lax.all_gather(pair, "chip", axis=0, tiled=False)
    earlier = lax.broadcasted_iota(jnp.int32, (nchip, 1, 1, 1), 0) < chip
    terms = jnp.where(earlier, pairs, eye[None])
    while terms.shape[0] > 1:
        terms = mm(terms[0::2], terms[1::2])
    before = terms[0]
    return jnp.where(core == 1, mm(before, partner), before)


def flash_attend(q_glob, kt_mine, kt_other, v_mine, v_other, shard, core, heads):
    rows, width = q_glob.shape
    nk = kt_mine.shape[0] * 2
    scale = 1.0 / math.sqrt(HDIM)

    def kernel(c_ref, q_ref, km_ref, ko_ref, vm_ref, vo_ref, o_ref, m_sc, l_sc, acc_sc):
        j = pl.program_id(0)
        c = c_ref[0]
        own = (j % 2) == c_ref[1]

        @pl.when(j == 0)
        def _():
            m_sc[...] = jnp.full(m_sc.shape, -1e30, jnp.float32)
            l_sc[...] = jnp.zeros(l_sc.shape, jnp.float32)
            acc_sc[...] = jnp.zeros(acc_sc.shape, jnp.float32)

        def step(k_ref, v_ref, masked):
            for hh in range(heads):
                sl = slice(hh * HDIM, (hh + 1) * HDIM)
                qh = q_ref[:, sl]
                kh = k_ref[sl, :]
                vh = v_ref[:, sl]
                s = jnp.dot(qh, kh, preferred_element_type=jnp.float32) * scale
                if masked:
                    row = lax.broadcasted_iota(jnp.int32, s.shape, 0)
                    col = lax.broadcasted_iota(jnp.int32, s.shape, 1)
                    allowed = col <= row
                    s = jnp.where(allowed, s, -1e30)
                m_prev = m_sc[hh]
                m_new = jnp.maximum(m_prev, jnp.max(s, axis=1, keepdims=True))
                p = jnp.exp(s - m_new)
                if masked:
                    p = jnp.where(allowed, p, 0.0)
                fade = jnp.exp(m_prev - m_new)
                l_sc[hh] = l_sc[hh] * fade + jnp.sum(p, axis=1, keepdims=True)
                acc_sc[hh] = acc_sc[hh] * fade + jnp.dot(
                    p.astype(jnp.bfloat16), vh, preferred_element_type=jnp.float32
                )
                m_sc[hh] = m_new

        @pl.when((j < c) & own)
        def _():
            step(km_ref, vm_ref, False)

        @pl.when((j < c) & jnp.logical_not(own))
        def _():
            step(ko_ref, vo_ref, False)

        @pl.when(j == c)
        def _():
            step(km_ref, vm_ref, True)

        @pl.when(j == nk - 1)
        def _():
            for hh in range(heads):
                sl = slice(hh * HDIM, (hh + 1) * HDIM)
                o_ref[:, sl] = (acc_sc[hh] / l_sc[hh]).astype(o_ref.dtype)

    def kv_block(j, c):
        return (jnp.minimum(j, c[0]) // 2, 0, 0)

    grid_spec = pltpu.PrefetchScalarGridSpec(
        num_scalar_prefetch=1,
        grid=(nk,),
        in_specs=[
            pl.BlockSpec((rows, width), lambda j, c: (0, 0)),
            pl.BlockSpec((None, width, rows), kv_block),
            pl.BlockSpec((None, width, rows), kv_block),
            pl.BlockSpec((None, rows, width), kv_block),
            pl.BlockSpec((None, rows, width), kv_block),
        ],
        out_specs=pl.BlockSpec((rows, width), lambda j, c: (0, 0)),
        scratch_shapes=[
            pltpu.VMEM((heads, rows, 1), jnp.float32),
            pltpu.VMEM((heads, rows, 1), jnp.float32),
            pltpu.VMEM((heads, rows, HDIM), jnp.float32),
        ],
    )
    where = jnp.stack([shard, core]).astype(jnp.int32)
    return pl.pallas_call(
        kernel,
        grid_spec=grid_spec,
        out_shape=jax.ShapeDtypeStruct((rows, width), jnp.bfloat16),
        compiler_params=pltpu.CompilerParams(dimension_semantics=("arbitrary",)),
    )(where, q_glob, kt_mine, kt_other, v_mine, v_other)


def local(queries, keys, values, reflect_ids, reflect_bank, out_weight):
    groups = lax.axis_size("hg")
    heads = reflect_ids.shape[1]
    width = heads * HDIM
    stacked = jnp.stack([queries, keys, values], axis=1).reshape(
        queries.shape[0], 3, groups, width
    )
    swapped = lax.all_to_all(stacked, "hg", split_axis=2, concat_axis=0, tiled=True)
    rows = swapped.shape[0]
    q_local = swapped[:, 0, 0]
    k_local = swapped[:, 1, 0]
    v_local = swapped[:, 2, 0]
    v_mine, v_other = chip_gather(v_local)

    nblocks = rows // BLK
    bank = reflect_bank.shape[0]
    table = reflect_bank.reshape(bank, heads, HDIM).transpose(1, 0, 2)
    onehot = (
        reflect_ids.T[:, :, None] == lax.broadcasted_iota(jnp.int32, (1, 1, bank), 2)
    ).astype(reflect_bank.dtype)
    chosen = jnp.einsum(
        "htb,hbd->htd", onehot, table, preferred_element_type=jnp.float32
    )
    vectors = chosen * lax.rsqrt(jnp.sum(chosen * chosen, axis=-1, keepdims=True) + 1e-06)
    blocks = vectors.reshape(heads, nblocks, BLK, HDIM)
    gram = jnp.einsum("hnkd,hnjd->hnkj", blocks, blocks, precision=HP)
    coupling = 2.0 * jnp.triu(gram, 1)
    tri_factor = 2.0 * invert_unit_upper(coupling)
    spread = jnp.einsum("hnkj,hnje->hnke", tri_factor, blocks, precision=HP)
    eye_d = jnp.eye(HDIM, dtype=jnp.float32)
    block_mats = eye_d - jnp.einsum("hnkd,hnke->hnde", blocks, spread, precision=HP)
    lower_mask = jnp.tril(jnp.ones((BLK, BLK), dtype=jnp.bool_))

    inner_prefix, shard_prod = exclusive_blocks(block_mats)
    earlier_prod = exclusive_shards(shard_prod)

    def in_shard(matrix):
        split = matrix.astype(jnp.float32).reshape(nblocks, BLK, heads, HDIM).transpose(2, 0, 1, 3)
        proj = jnp.einsum("hnid,hnkd->hnik", split, blocks, precision=HP)
        proj = jnp.where(lower_mask, proj, 0.0)
        coef = jnp.einsum("hnik,hnrk->hnir", proj, tri_factor, precision=HP)
        inblock = split - jnp.einsum("hnir,hnrd->hnid", coef, blocks, precision=HP)
        moved = jnp.einsum("hnid,hned->hnie", inblock, inner_prefix, precision=HP)
        return moved.reshape(heads, rows, HDIM)

    kt_glob = jnp.einsum(
        "hie,hfe->hfi", in_shard(k_local), earlier_prod, precision=HP
    ).reshape(width, rows).astype(jnp.bfloat16)
    kt_mine, kt_other = chip_gather(kt_glob)
    q_glob = (
        jnp.einsum("hie,hfe->hif", in_shard(q_local), earlier_prod, precision=HP)
        .transpose(1, 0, 2)
        .reshape(rows, width)
        .astype(jnp.bfloat16)
    )

    core = lax.axis_index("core")
    shard = lax.axis_index("chip") * 2 + core
    attn = flash_attend(q_glob, kt_mine, kt_other, v_mine, v_other, shard, core, heads)
    return lax.psum_scatter(
        jnp.dot(attn, out_weight, preferred_element_type=jnp.float32).astype(jnp.bfloat16),
        "hg",
        scatter_dimension=0,
        tiled=True,
    )


def solution(mesh):
    nctx, ngroups = mesh.shape["ctx"], mesh.shape["hg"]
    split = jax.sharding.Mesh(
        mesh.devices.reshape(nctx // 2, 2, ngroups), ("chip", "core", "hg")
    )
    ctx = ("chip", "core")
    placed = (
        P((*ctx, "hg"), None),
        P((*ctx, "hg"), None),
        P((*ctx, "hg"), None),
        P(ctx, "hg"),
        P(None, "hg"),
        P("hg", None),
    )
    return jax.shard_map(
        local, mesh=split, in_specs=placed, out_specs=P((*ctx, "hg"), None), check_vma=False
    )
```

```python
import math

import jax
import jax.numpy as jnp
from jax import lax
from jax.experimental import pallas as pl
from jax.experimental.pallas import tpu as pltpu
from jax.sharding import PartitionSpec as P

HDIM = 128
BLK = 32
HP = lax.Precision.HIGHEST


def mm(a, b):
    return jnp.einsum("...ij,...jk->...ik", a, b, precision=HP)


def invert_unit_upper(strict):
    eye_blk = jnp.eye(strict.shape[-1], dtype=jnp.float32)
    result = eye_blk - strict
    power = strict
    steps = strict.shape[-1].bit_length()
    for level in range(steps):
        power = mm(power, power)
        result = mm(result, eye_blk + power)
    return result


def exclusive_blocks(mats):
    heads, n, d, _ = mats.shape
    eye = jnp.broadcast_to(jnp.eye(d, dtype=jnp.float32), (heads, 1, d, d))
    acc = jnp.concatenate([eye, mats[:, :-1]], axis=1)
    shift = 1
    while shift < n:
        earlier = jnp.concatenate(
            [jnp.broadcast_to(eye, (heads, shift, d, d)), acc[:, : n - shift]], axis=1
        )
        acc = mm(earlier, acc)
        shift *= 2
    return acc, mm(acc[:, -1], mats[:, -1])


def exclusive_shards(mat, axis):
    length, here = lax.axis_size(axis), lax.axis_index(axis)
    eye = jnp.broadcast_to(jnp.eye(mat.shape[-1], dtype=jnp.float32), mat.shape)
    if length == 1:
        return eye
    acc = lax.ppermute(mat, axis, [(i, i + 1) for i in range(length - 1)])
    acc = jnp.where(here >= 1, acc, eye)
    shift = 1
    while shift < length:
        earlier = lax.ppermute(acc, axis, [(i, i + shift) for i in range(length - shift)])
        acc = jnp.where(here >= shift, mm(earlier, acc), acc)
        shift *= 2
    return acc


def flash_attend(q_glob, kt_all, v_all, part, shard, heads):
    rows, width = q_glob.shape
    nk = kt_all.shape[0]
    scale = 1.0 / math.sqrt(HDIM)

    def kernel(c_ref, q_ref, k_ref, v_ref, o_ref, m_sc, l_sc, acc_sc):
        j = pl.program_id(0)
        c = c_ref[0]

        @pl.when(j == 0)
        def _():
            m_sc[...] = jnp.full(m_sc.shape, -1e30, jnp.float32)
            l_sc[...] = jnp.zeros(l_sc.shape, jnp.float32)
            acc_sc[...] = jnp.zeros(acc_sc.shape, jnp.float32)

        def step(masked):
            for hh in range(heads):
                sl = slice(hh * HDIM, (hh + 1) * HDIM)
                qh = q_ref[:, sl]
                kh = k_ref[sl, :]
                vh = v_ref[:, sl]
                s = jnp.dot(qh, kh, preferred_element_type=jnp.float32) * scale
                if masked:
                    row = lax.broadcasted_iota(jnp.int32, s.shape, 0)
                    col = lax.broadcasted_iota(jnp.int32, s.shape, 1)
                    allowed = col <= row
                    s = jnp.where(allowed, s, -1e30)
                m_prev = m_sc[hh]
                m_new = jnp.maximum(m_prev, jnp.max(s, axis=1, keepdims=True))
                p = jnp.exp(s - m_new)
                if masked:
                    p = jnp.where(allowed, p, 0.0)
                fade = jnp.exp(m_prev - m_new)
                l_sc[hh] = l_sc[hh] * fade + jnp.sum(p, axis=1, keepdims=True)
                acc_sc[hh] = acc_sc[hh] * fade + jnp.dot(
                    p.astype(jnp.bfloat16), vh, preferred_element_type=jnp.float32
                )
                m_sc[hh] = m_new

        @pl.when(j < c)
        def _():
            step(False)

        @pl.when(j == c)
        def _():
            step(True)

        @pl.when(j == nk - 1)
        def _():
            for hh in range(heads):
                sl = slice(hh * HDIM, (hh + 1) * HDIM)
                o_ref[:, sl] = (acc_sc[hh] / l_sc[hh]).astype(o_ref.dtype)

    grid_spec = pltpu.PrefetchScalarGridSpec(
        num_scalar_prefetch=1,
        grid=(nk,),
        in_specs=[
            pl.BlockSpec((rows, width), lambda j, c: (0, 0)),
            pl.BlockSpec((None, width, rows), lambda j, c: (jnp.minimum(j, c[0]), 0, 0)),
            pl.BlockSpec((None, rows, width), lambda j, c: (jnp.minimum(j, c[0]), 0, part)),
        ],
        out_specs=pl.BlockSpec((rows, width), lambda j, c: (0, 0)),
        scratch_shapes=[
            pltpu.VMEM((heads, rows, 1), jnp.float32),
            pltpu.VMEM((heads, rows, 1), jnp.float32),
            pltpu.VMEM((heads, rows, HDIM), jnp.float32),
        ],
    )
    return pl.pallas_call(
        kernel,
        grid_spec=grid_spec,
        out_shape=jax.ShapeDtypeStruct((rows, width), jnp.bfloat16),
        compiler_params=pltpu.CompilerParams(dimension_semantics=("arbitrary",)),
    )(jnp.reshape(shard, (1,)).astype(jnp.int32), q_glob, kt_all, v_all)


SWAP = [(0, 1), (1, 0)]


def exchange_heads(stacked, groups):
    if groups != 2:
        return lax.all_to_all(stacked, "hg", split_axis=2, concat_axis=0, tiled=True)[:, :, 0]
    first = lax.axis_index("hg") == 0
    own = jnp.where(first, stacked[:, :, 0], stacked[:, :, 1])
    got = lax.ppermute(jnp.where(first, stacked[:, :, 1], stacked[:, :, 0]), "hg", SWAP)
    return jnp.where(
        first, jnp.concatenate([own, got], axis=0), jnp.concatenate([got, own], axis=0)
    )


def project_out(attn, out_weight, groups):
    if groups != 2:
        return lax.psum_scatter(
            jnp.dot(attn, out_weight, preferred_element_type=jnp.float32).astype(jnp.bfloat16),
            "hg",
            scatter_dimension=0,
            tiled=True,
        )
    half = attn.shape[0] // 2
    first = lax.axis_index("hg") == 0
    theirs = jnp.where(first, attn[half:], attn[:half])
    mine = jnp.where(first, attn[:half], attn[half:])
    sent = jnp.dot(theirs, out_weight, preferred_element_type=jnp.float32).astype(jnp.bfloat16)
    got = lax.ppermute(sent, "hg", SWAP)
    kept = jnp.dot(mine, out_weight, preferred_element_type=jnp.float32)
    return (kept + got.astype(jnp.float32)).astype(jnp.bfloat16)


def local(queries, keys, values, reflect_ids, reflect_bank, out_weight):
    groups = lax.axis_size("hg")
    heads = reflect_ids.shape[1]
    width = heads * HDIM
    stacked = jnp.stack([queries, keys, values], axis=1).reshape(
        queries.shape[0], 3, groups, width
    )
    swapped, reflect_ids = lax.optimization_barrier((exchange_heads(stacked, groups), reflect_ids))
    rows = swapped.shape[0]
    q_local = swapped[:, 0]
    k_local = swapped[:, 1]
    v_local = swapped[:, 2]
    v_all = lax.all_gather(v_local, "ctx", axis=0, tiled=False)

    nblocks = rows // BLK
    bank = reflect_bank.shape[0]
    table = reflect_bank.reshape(bank, heads, HDIM).transpose(1, 0, 2)
    onehot = (
        reflect_ids.T[:, :, None] == lax.broadcasted_iota(jnp.int32, (1, 1, bank), 2)
    ).astype(reflect_bank.dtype)
    chosen = jnp.einsum(
        "htb,hbd->htd", onehot, table, preferred_element_type=jnp.float32
    )
    vectors = chosen * lax.rsqrt(jnp.sum(chosen * chosen, axis=-1, keepdims=True) + 1e-06)
    blocks = vectors.reshape(heads, nblocks, BLK, HDIM)
    gram = jnp.einsum("hnkd,hnjd->hnkj", blocks, blocks, precision=HP)
    coupling = 2.0 * jnp.triu(gram, 1)
    tri_factor = 2.0 * invert_unit_upper(coupling)
    spread = jnp.einsum("hnkj,hnje->hnke", tri_factor, blocks, precision=HP)
    eye_d = jnp.eye(HDIM, dtype=jnp.float32)
    block_mats = eye_d - jnp.einsum("hnkd,hnke->hnde", blocks, spread, precision=HP)
    lower_mask = jnp.tril(jnp.ones((BLK, BLK), dtype=jnp.bool_))

    inner_prefix, shard_prod = exclusive_blocks(block_mats)
    earlier_prod, v_all = lax.optimization_barrier((exclusive_shards(shard_prod, "ctx"), v_all))

    def in_shard(matrix):
        split = matrix.astype(jnp.float32).reshape(nblocks, BLK, heads, HDIM).transpose(2, 0, 1, 3)
        proj = jnp.einsum("hnid,hnkd->hnik", split, blocks, precision=HP)
        proj = jnp.where(lower_mask, proj, 0.0)
        coef = jnp.einsum("hnik,hnrk->hnir", proj, tri_factor, precision=HP)
        inblock = split - jnp.einsum("hnir,hnrd->hnid", coef, blocks, precision=HP)
        moved = jnp.einsum("hnid,hned->hnie", inblock, inner_prefix, precision=HP)
        return moved.reshape(heads, rows, HDIM)

    kt_glob = jnp.einsum(
        "hie,hfe->hfi", in_shard(k_local), earlier_prod, precision=HP
    ).reshape(width, rows).astype(jnp.bfloat16)
    parts = 2 if heads % 2 == 0 else 1
    pw = width // parts
    kt_parts = [
        lax.all_gather(kt_glob[p * pw : (p + 1) * pw], "ctx", axis=0, tiled=False)
        for p in range(parts)
    ]
    q_glob = (
        jnp.einsum("hie,hfe->hif", in_shard(q_local), earlier_prod, precision=HP)
        .transpose(1, 0, 2)
        .reshape(rows, width)
        .astype(jnp.bfloat16)
    )
    shard = lax.axis_index("ctx")
    attn = jnp.concatenate(
        [
            flash_attend(q_glob[:, p * pw : (p + 1) * pw], kt_parts[p], v_all, p, shard, heads // parts)
            for p in range(parts)
        ],
        axis=1,
    )
    return project_out(attn, out_weight, groups)


def solution(mesh):
    placed = (
        P(("ctx", "hg"), None),
        P(("ctx", "hg"), None),
        P(("ctx", "hg"), None),
        P("ctx", "hg"),
        P(None, "hg"),
        P("hg", None),
    )
    return jax.shard_map(
        local, mesh=mesh, in_specs=placed, out_specs=P(("ctx", "hg"), None), check_vma=False
    )
```

```python
import math

import jax
import jax.numpy as jnp
from jax import lax
from jax.experimental import pallas as pl
from jax.experimental.pallas import tpu as pltpu
from jax.sharding import PartitionSpec as P

HDIM = 128
BLK = 32
GROUP = 1
HP = lax.Precision.HIGHEST


def mm(a, b):
    return jnp.einsum("...ij,...jk->...ik", a, b, precision=HP)


def invert_unit_upper(strict):
    eye_blk = jnp.eye(strict.shape[-1], dtype=jnp.float32)
    result = eye_blk - strict
    power = strict
    steps = strict.shape[-1].bit_length()
    for level in range(steps):
        power = mm(power, power)
        result = mm(result, eye_blk + power)
    return result


def exclusive_blocks(mats):
    heads, n, d, _ = mats.shape
    eye = jnp.broadcast_to(jnp.eye(d, dtype=jnp.float32), (heads, 1, d, d))
    acc = jnp.concatenate([eye, mats[:, :-1]], axis=1)
    shift = 1
    while shift < n:
        earlier = jnp.concatenate(
            [jnp.broadcast_to(eye, (heads, shift, d, d)), acc[:, : n - shift]], axis=1
        )
        acc = mm(earlier, acc)
        shift *= 2
    return acc, mm(acc[:, -1], mats[:, -1])


def exclusive_shards(mat, axis):
    length, here = lax.axis_size(axis), lax.axis_index(axis)
    eye = jnp.broadcast_to(jnp.eye(mat.shape[-1], dtype=jnp.float32), mat.shape)
    if length == 1:
        return eye
    acc = lax.ppermute(mat, axis, [(i, i + 1) for i in range(length - 1)])
    acc = jnp.where(here >= 1, acc, eye)
    shift = 1
    while shift < length:
        earlier = lax.ppermute(acc, axis, [(i, i + shift) for i in range(length - shift)])
        acc = jnp.where(here >= shift, mm(earlier, acc), acc)
        shift *= 2
    return acc


def flash_attend(q_glob, kt_all, v_all, part, shard, heads, group=GROUP):
    rows, width = q_glob.shape
    nk = kt_all.shape[0]
    while nk % group:
        group //= 2
    nb = nk // group
    scale = 1.0 / math.sqrt(HDIM)

    def kernel(c_ref, q_ref, k_ref, v_ref, o_ref, m_sc, l_sc, acc_sc):
        j = pl.program_id(0)
        c = c_ref[0]

        @pl.when(j == 0)
        def _():
            m_sc[...] = jnp.full(m_sc.shape, -1e30, jnp.float32)
            l_sc[...] = jnp.zeros(l_sc.shape, jnp.float32)
            acc_sc[...] = jnp.zeros(acc_sc.shape, jnp.float32)

        def step(g, masked):
            for hh in range(heads):
                sl = slice(hh * HDIM, (hh + 1) * HDIM)
                qh = q_ref[:, sl]
                kh = k_ref[g, sl, :]
                vh = v_ref[g, :, sl]
                s = jnp.dot(qh, kh, preferred_element_type=jnp.float32) * scale
                if masked:
                    row = lax.broadcasted_iota(jnp.int32, s.shape, 0)
                    col = lax.broadcasted_iota(jnp.int32, s.shape, 1)
                    allowed = col <= row
                    s = jnp.where(allowed, s, -1e30)
                m_prev = m_sc[hh]
                m_new = jnp.maximum(m_prev, jnp.max(s, axis=1, keepdims=True))
                if s.shape[1] % HDIM == 0:
                    wide = jnp.concatenate([m_new] * (s.shape[1] // HDIM), axis=1)
                else:
                    wide = m_new[:, :1]
                p = jnp.exp(s - wide)
                if masked:
                    p = jnp.where(allowed, p, 0.0)
                fade = jnp.exp(m_prev - m_new)
                l_sc[hh] = l_sc[hh] * fade + jnp.sum(p, axis=1, keepdims=True)
                acc_sc[hh] = acc_sc[hh] * fade + jnp.dot(
                    p.astype(jnp.bfloat16), vh, preferred_element_type=jnp.float32
                )
                m_sc[hh] = m_new

        for g in range(group):
            here = j * group + g

            @pl.when(here < c)
            def _():
                step(g, False)

            @pl.when(here == c)
            def _():
                step(g, True)

        @pl.when(j == nb - 1)
        def _():
            for hh in range(heads):
                sl = slice(hh * HDIM, (hh + 1) * HDIM)
                o_ref[:, sl] = (acc_sc[hh] / l_sc[hh]).astype(o_ref.dtype)

    grid_spec = pltpu.PrefetchScalarGridSpec(
        num_scalar_prefetch=1,
        grid=(nb,),
        in_specs=[
            pl.BlockSpec((rows, width), lambda j, c: (0, 0)),
            pl.BlockSpec((group, width, rows), lambda j, c: (jnp.minimum(j, c[0] // group), 0, 0)),
            pl.BlockSpec((group, rows, width), lambda j, c: (jnp.minimum(j, c[0] // group), 0, part)),
        ],
        out_specs=pl.BlockSpec((rows, width), lambda j, c: (0, 0)),
        scratch_shapes=[
            pltpu.VMEM((heads, rows, HDIM), jnp.float32),
            pltpu.VMEM((heads, rows, HDIM), jnp.float32),
            pltpu.VMEM((heads, rows, HDIM), jnp.float32),
        ],
    )
    return pl.pallas_call(
        kernel,
        grid_spec=grid_spec,
        out_shape=jax.ShapeDtypeStruct((rows, width), jnp.bfloat16),
        compiler_params=pltpu.CompilerParams(dimension_semantics=("arbitrary",)),
    )(jnp.reshape(shard, (1,)).astype(jnp.int32), q_glob, kt_all, v_all)


SWAP = [(0, 1), (1, 0)]


def exchange_heads(stacked, groups):
    if groups != 2:
        return lax.all_to_all(stacked, "hg", split_axis=2, concat_axis=0, tiled=True)[:, :, 0]
    first = lax.axis_index("hg") == 0
    own = jnp.where(first, stacked[:, :, 0], stacked[:, :, 1])
    got = lax.ppermute(jnp.where(first, stacked[:, :, 1], stacked[:, :, 0]), "hg", SWAP)
    return jnp.where(
        first, jnp.concatenate([own, got], axis=0), jnp.concatenate([got, own], axis=0)
    )


def project_out(attn, out_weight, groups):
    if groups != 2:
        return lax.psum_scatter(
            jnp.dot(attn, out_weight, preferred_element_type=jnp.float32).astype(jnp.bfloat16),
            "hg",
            scatter_dimension=0,
            tiled=True,
        )
    half = attn.shape[0] // 2
    first = lax.axis_index("hg") == 0
    theirs = jnp.where(first, attn[half:], attn[:half])
    mine = jnp.where(first, attn[:half], attn[half:])
    sent = jnp.dot(theirs, out_weight, preferred_element_type=jnp.float32).astype(jnp.bfloat16)
    got = lax.ppermute(sent, "hg", SWAP)
    kept = jnp.dot(mine, out_weight, preferred_element_type=jnp.float32)
    return (kept + got.astype(jnp.float32)).astype(jnp.bfloat16)


def local(queries, keys, values, reflect_ids, reflect_bank, out_weight):
    groups = lax.axis_size("hg")
    heads = reflect_ids.shape[1]
    width = heads * HDIM
    stacked = jnp.stack([queries, keys, values], axis=1).reshape(
        queries.shape[0], 3, groups, width
    )
    swapped, reflect_ids = lax.optimization_barrier((exchange_heads(stacked, groups), reflect_ids))
    rows = swapped.shape[0]
    q_local = swapped[:, 0]
    k_local = swapped[:, 1]
    v_local = swapped[:, 2]
    v_all = lax.all_gather(v_local, "ctx", axis=0, tiled=False)

    nblocks = rows // BLK
    bank = reflect_bank.shape[0]
    table = reflect_bank.reshape(bank, heads, HDIM).transpose(1, 0, 2)
    onehot = (
        reflect_ids.T[:, :, None] == lax.broadcasted_iota(jnp.int32, (1, 1, bank), 2)
    ).astype(reflect_bank.dtype)
    chosen = jnp.einsum(
        "htb,hbd->htd", onehot, table, preferred_element_type=jnp.float32
    )
    vectors = chosen * lax.rsqrt(jnp.sum(chosen * chosen, axis=-1, keepdims=True) + 1e-06)
    blocks = vectors.reshape(heads, nblocks, BLK, HDIM)
    gram = jnp.einsum("hnkd,hnjd->hnkj", blocks, blocks, precision=HP)
    coupling = 2.0 * jnp.triu(gram, 1)
    tri_factor = 2.0 * invert_unit_upper(coupling)
    spread = jnp.einsum("hnkj,hnje->hnke", tri_factor, blocks, precision=HP)
    eye_d = jnp.eye(HDIM, dtype=jnp.float32)
    block_mats = eye_d - jnp.einsum("hnkd,hnke->hnde", blocks, spread, precision=HP)
    lower_mask = jnp.tril(jnp.ones((BLK, BLK), dtype=jnp.bool_))

    inner_prefix, shard_prod = exclusive_blocks(block_mats)
    earlier_prod, v_all = lax.optimization_barrier((exclusive_shards(shard_prod, "ctx"), v_all))

    def in_shard(matrix):
        split = matrix.astype(jnp.float32).reshape(nblocks, BLK, heads, HDIM).transpose(2, 0, 1, 3)
        proj = jnp.einsum("hnid,hnkd->hnik", split, blocks, precision=HP)
        proj = jnp.where(lower_mask, proj, 0.0)
        coef = jnp.einsum("hnik,hnrk->hnir", proj, tri_factor, precision=HP)
        inblock = split - jnp.einsum("hnir,hnrd->hnid", coef, blocks, precision=HP)
        moved = jnp.einsum("hnid,hned->hnie", inblock, inner_prefix, precision=HP)
        return moved.reshape(heads, rows, HDIM)

    kt_glob = jnp.einsum(
        "hie,hfe->hfi", in_shard(k_local), earlier_prod, precision=HP
    ).reshape(width, rows).astype(jnp.bfloat16)
    parts = 2 if heads % 2 == 0 else 1
    pw = width // parts
    kt_parts = [
        lax.all_gather(kt_glob[p * pw : (p + 1) * pw], "ctx", axis=0, tiled=False)
        for p in range(parts)
    ]
    q_glob = (
        jnp.einsum("hie,hfe->hif", in_shard(q_local), earlier_prod, precision=HP)
        .transpose(1, 0, 2)
        .reshape(rows, width)
        .astype(jnp.bfloat16)
    )
    shard = lax.axis_index("ctx")
    attn = jnp.concatenate(
        [
            flash_attend(q_glob[:, p * pw : (p + 1) * pw], kt_parts[p], v_all, p, shard, heads // parts)
            for p in range(parts)
        ],
        axis=1,
    )
    return project_out(attn, out_weight, groups)


def solution(mesh):
    placed = (
        P(("ctx", "hg"), None),
        P(("ctx", "hg"), None),
        P(("ctx", "hg"), None),
        P("ctx", "hg"),
        P(None, "hg"),
        P("hg", None),
    )
    return jax.shard_map(
        local, mesh=mesh, in_specs=placed, out_specs=P(("ctx", "hg"), None), check_vma=False
    )
```

```python
import math

import jax
import jax.numpy as jnp
from jax import lax
from jax.experimental import pallas as pl
from jax.experimental.pallas import tpu as pltpu
from jax.sharding import PartitionSpec as P

HDIM = 128
BLK = 32
GROUP = 1
HP = lax.Precision.HIGHEST


def mm(a, b):
    return jnp.einsum("...ij,...jk->...ik", a, b, precision=HP)


def invert_unit_upper(strict):
    eye_blk = jnp.eye(strict.shape[-1], dtype=jnp.float32)
    result = eye_blk - strict
    power = strict
    steps = strict.shape[-1].bit_length()
    for level in range(steps):
        power = mm(power, power)
        result = mm(result, eye_blk + power)
    return result


def exclusive_blocks(mats):
    heads, n, d, _ = mats.shape
    eye = jnp.broadcast_to(jnp.eye(d, dtype=jnp.float32), (heads, 1, d, d))
    acc = jnp.concatenate([eye, mats[:, :-1]], axis=1)
    shift = 1
    while shift < n:
        earlier = jnp.concatenate(
            [jnp.broadcast_to(eye, (heads, shift, d, d)), acc[:, : n - shift]], axis=1
        )
        acc = mm(earlier, acc)
        shift *= 2
    return acc, mm(acc[:, -1], mats[:, -1])


def exclusive_shards(mat, axis):
    length, here = lax.axis_size(axis), lax.axis_index(axis)
    eye = jnp.broadcast_to(jnp.eye(mat.shape[-1], dtype=jnp.float32), mat.shape)
    if length == 1:
        return eye
    acc = lax.ppermute(mat, axis, [(i, i + 1) for i in range(length - 1)])
    acc = jnp.where(here >= 1, acc, eye)
    shift = 1
    while shift < length:
        earlier = lax.ppermute(acc, axis, [(i, i + shift) for i in range(length - shift)])
        acc = jnp.where(here >= shift, mm(earlier, acc), acc)
        shift *= 2
    return acc


def flash_attend(q_glob, kt_all, v_all, part, shard, heads, group=GROUP):
    rows, width = q_glob.shape
    nk = kt_all.shape[0]
    while nk % group:
        group //= 2
    nb = nk // group
    scale = 1.0 / math.sqrt(HDIM)

    def kernel(c_ref, q_ref, k_ref, v_ref, o_ref, m_sc, l_sc, acc_sc):
        j = pl.program_id(0)
        c = c_ref[0]

        @pl.when(j == 0)
        def _():
            m_sc[...] = jnp.full(m_sc.shape, -1e30, jnp.float32)
            l_sc[...] = jnp.zeros(l_sc.shape, jnp.float32)
            acc_sc[...] = jnp.zeros(acc_sc.shape, jnp.float32)

        def step(g, masked):
            for hh in range(heads):
                sl = slice(hh * HDIM, (hh + 1) * HDIM)
                qh = q_ref[:, sl]
                kh = k_ref[g, sl, :]
                vh = v_ref[g, :, sl]
                s = jnp.dot(qh, kh, preferred_element_type=jnp.float32) * scale
                if masked:
                    row = lax.broadcasted_iota(jnp.int32, s.shape, 0)
                    col = lax.broadcasted_iota(jnp.int32, s.shape, 1)
                    allowed = col <= row
                    s = jnp.where(allowed, s, -1e30)
                m_prev = m_sc[hh]
                m_new = jnp.maximum(m_prev, jnp.max(s, axis=1, keepdims=True))
                if s.shape[1] % HDIM == 0:
                    wide = jnp.concatenate([m_new] * (s.shape[1] // HDIM), axis=1)
                else:
                    wide = m_new[:, :1]
                p = jnp.exp(s - wide)
                if masked:
                    p = jnp.where(allowed, p, 0.0)
                fade = jnp.exp(m_prev - m_new)
                l_sc[hh] = l_sc[hh] * fade + jnp.sum(p, axis=1, keepdims=True)
                acc_sc[hh] = acc_sc[hh] * fade + jnp.dot(
                    p.astype(jnp.bfloat16), vh, preferred_element_type=jnp.float32
                )
                m_sc[hh] = m_new

        for g in range(group):
            here = j * group + g

            @pl.when(here < c)
            def _():
                step(g, False)

            @pl.when(here == c)
            def _():
                step(g, True)

        @pl.when(j == nb - 1)
        def _():
            for hh in range(heads):
                sl = slice(hh * HDIM, (hh + 1) * HDIM)
                o_ref[:, sl] = (acc_sc[hh] / l_sc[hh]).astype(o_ref.dtype)

    grid_spec = pltpu.PrefetchScalarGridSpec(
        num_scalar_prefetch=1,
        grid=(nb,),
        in_specs=[
            pl.BlockSpec((rows, width), lambda j, c: (0, 0)),
            pl.BlockSpec((group, width, rows), lambda j, c: (jnp.minimum(j, c[0] // group), 0, 0)),
            pl.BlockSpec((group, rows, width), lambda j, c: (jnp.minimum(j, c[0] // group), 0, part)),
        ],
        out_specs=pl.BlockSpec((rows, width), lambda j, c: (0, 0)),
        scratch_shapes=[
            pltpu.VMEM((heads, rows, HDIM), jnp.float32),
            pltpu.VMEM((heads, rows, HDIM), jnp.float32),
            pltpu.VMEM((heads, rows, HDIM), jnp.float32),
        ],
    )
    return pl.pallas_call(
        kernel,
        grid_spec=grid_spec,
        out_shape=jax.ShapeDtypeStruct((rows, width), jnp.bfloat16),
        compiler_params=pltpu.CompilerParams(dimension_semantics=("arbitrary",)),
    )(jnp.reshape(shard, (1,)).astype(jnp.int32), q_glob, kt_all, v_all)


SWAP = [(0, 1), (1, 0)]


def exchange_heads(stacked, groups):
    if groups != 2:
        return lax.all_to_all(stacked, "hg", split_axis=2, concat_axis=0, tiled=True)[:, :, 0]
    first = lax.axis_index("hg") == 0
    own = jnp.where(first, stacked[:, :, 0], stacked[:, :, 1])
    got = lax.ppermute(jnp.where(first, stacked[:, :, 1], stacked[:, :, 0]), "hg", SWAP)
    return jnp.where(
        first, jnp.concatenate([own, got], axis=0), jnp.concatenate([got, own], axis=0)
    )


def project_out(parts, out_weight, w_other, groups):
    if groups != 2:
        return lax.psum_scatter(
            jnp.dot(
                jnp.concatenate(parts, axis=1), out_weight, preferred_element_type=jnp.float32
            ).astype(jnp.bfloat16),
            "hg",
            scatter_dimension=0,
            tiled=True,
        )
    half = parts[0].shape[0] // 2
    first = lax.axis_index("hg") == 0
    got = [
        lax.ppermute(jnp.where(first, a[half:], a[:half]), "hg", SWAP) for a in parts
    ]
    mine = jnp.concatenate([jnp.where(first, a[:half], a[half:]) for a in parts], axis=1)
    total = jnp.dot(mine, out_weight, preferred_element_type=jnp.float32)
    pw = parts[0].shape[1]
    for p, a in enumerate(got):
        total = total + jnp.dot(
            a, w_other[p * pw : (p + 1) * pw], preferred_element_type=jnp.float32
        )
    return total.astype(jnp.bfloat16)


def local(queries, keys, values, reflect_ids, reflect_bank, out_weight):
    groups = lax.axis_size("hg")
    heads = reflect_ids.shape[1]
    width = heads * HDIM
    stacked = jnp.stack([queries, keys, values], axis=1).reshape(
        queries.shape[0], 3, groups, width
    )
    swapped, reflect_ids = lax.optimization_barrier((exchange_heads(stacked, groups), reflect_ids))
    rows = swapped.shape[0]
    q_local = swapped[:, 0]
    k_local = swapped[:, 1]
    v_local = swapped[:, 2]
    v_all = lax.all_gather(v_local, "ctx", axis=0, tiled=False)

    nblocks = rows // BLK
    bank = reflect_bank.shape[0]
    table = reflect_bank.reshape(bank, heads, HDIM).transpose(1, 0, 2)
    onehot = (
        reflect_ids.T[:, :, None] == lax.broadcasted_iota(jnp.int32, (1, 1, bank), 2)
    ).astype(reflect_bank.dtype)
    chosen = jnp.einsum(
        "htb,hbd->htd", onehot, table, preferred_element_type=jnp.float32
    )
    vectors = chosen * lax.rsqrt(jnp.sum(chosen * chosen, axis=-1, keepdims=True) + 1e-06)
    blocks = vectors.reshape(heads, nblocks, BLK, HDIM)
    gram = jnp.einsum("hnkd,hnjd->hnkj", blocks, blocks, precision=HP)
    coupling = 2.0 * jnp.triu(gram, 1)
    tri_factor = 2.0 * invert_unit_upper(coupling)
    spread = jnp.einsum("hnkj,hnje->hnke", tri_factor, blocks, precision=HP)
    eye_d = jnp.eye(HDIM, dtype=jnp.float32)
    block_mats = eye_d - jnp.einsum("hnkd,hnke->hnde", blocks, spread, precision=HP)
    lower_mask = jnp.tril(jnp.ones((BLK, BLK), dtype=jnp.bool_))

    inner_prefix, shard_prod = exclusive_blocks(block_mats)
    w_other = lax.ppermute(out_weight, "hg", SWAP) if groups == 2 else None
    earlier_prod, v_all, w_other = lax.optimization_barrier(
        (exclusive_shards(shard_prod, "ctx"), v_all, w_other)
    )

    def in_shard(matrix):
        split = matrix.astype(jnp.float32).reshape(nblocks, BLK, heads, HDIM).transpose(2, 0, 1, 3)
        proj = jnp.einsum("hnid,hnkd->hnik", split, blocks, precision=HP)
        proj = jnp.where(lower_mask, proj, 0.0)
        coef = jnp.einsum("hnik,hnrk->hnir", proj, tri_factor, precision=HP)
        inblock = split - jnp.einsum("hnir,hnrd->hnid", coef, blocks, precision=HP)
        moved = jnp.einsum("hnid,hned->hnie", inblock, inner_prefix, precision=HP)
        return moved.reshape(heads, rows, HDIM)

    kt_glob = jnp.einsum(
        "hie,hfe->hfi", in_shard(k_local), earlier_prod, precision=HP
    ).reshape(width, rows).astype(jnp.bfloat16)
    parts = 2 if heads % 2 == 0 else 1
    pw = width // parts
    kt_parts = [
        lax.all_gather(kt_glob[p * pw : (p + 1) * pw], "ctx", axis=0, tiled=False)
        for p in range(parts)
    ]
    q_glob = (
        jnp.einsum("hie,hfe->hif", in_shard(q_local), earlier_prod, precision=HP)
        .transpose(1, 0, 2)
        .reshape(rows, width)
        .astype(jnp.bfloat16)
    )
    shard = lax.axis_index("ctx")
    attn = [
        flash_attend(q_glob[:, p * pw : (p + 1) * pw], kt_parts[p], v_all, p, shard, heads // parts)
        for p in range(parts)
    ]
    return project_out(attn, out_weight, w_other, groups)


def solution(mesh):
    placed = (
        P(("ctx", "hg"), None),
        P(("ctx", "hg"), None),
        P(("ctx", "hg"), None),
        P("ctx", "hg"),
        P(None, "hg"),
        P("hg", None),
    )
    return jax.shard_map(
        local, mesh=mesh, in_specs=placed, out_specs=P(("ctx", "hg"), None), check_vma=False
    )
```

```python
import math

import jax
import jax.numpy as jnp
from jax import lax
from jax.experimental import pallas as pl
from jax.experimental.pallas import tpu as pltpu
from jax.sharding import PartitionSpec as P

HDIM = 128
BLK = 32
GROUP = 1
HP = lax.Precision.HIGHEST


def mm(a, b):
    return jnp.einsum("...ij,...jk->...ik", a, b, precision=HP)


def invert_unit_upper(strict):
    eye_blk = jnp.eye(strict.shape[-1], dtype=jnp.float32)
    result = eye_blk - strict
    power = strict
    steps = strict.shape[-1].bit_length()
    for level in range(steps):
        power = mm(power, power)
        result = mm(result, eye_blk + power)
    return result


def exclusive_blocks(mats):
    heads, n, d, _ = mats.shape
    eye = jnp.broadcast_to(jnp.eye(d, dtype=jnp.float32), (heads, 1, d, d))
    acc = jnp.concatenate([eye, mats[:, :-1]], axis=1)
    shift = 1
    while shift < n:
        earlier = jnp.concatenate(
            [jnp.broadcast_to(eye, (heads, shift, d, d)), acc[:, : n - shift]], axis=1
        )
        acc = mm(earlier, acc)
        shift *= 2
    return acc, mm(acc[:, -1], mats[:, -1])


def exclusive_shards(mat, axis):
    length, here = lax.axis_size(axis), lax.axis_index(axis)
    eye = jnp.broadcast_to(jnp.eye(mat.shape[-1], dtype=jnp.float32), mat.shape)
    if length == 1:
        return eye
    acc = lax.ppermute(mat, axis, [(i, i + 1) for i in range(length - 1)])
    acc = jnp.where(here >= 1, acc, eye)
    shift = 1
    while shift < length:
        earlier = lax.ppermute(acc, axis, [(i, i + shift) for i in range(length - shift)])
        acc = jnp.where(here >= shift, mm(earlier, acc), acc)
        shift *= 2
    return acc


def flash_attend(q_glob, kt_all, v_all, part, shard, heads, group=GROUP):
    rows, width = q_glob.shape
    nk = kt_all.shape[0]
    while nk % group:
        group //= 2
    nb = nk // group
    scale = 1.0 / math.sqrt(HDIM)

    def kernel(c_ref, q_ref, k_ref, v_ref, o_ref, m_sc, l_sc, acc_sc):
        j = pl.program_id(0)
        c = c_ref[0]

        @pl.when(j == 0)
        def _():
            m_sc[...] = jnp.full(m_sc.shape, -1e30, jnp.float32)
            l_sc[...] = jnp.zeros(l_sc.shape, jnp.float32)
            acc_sc[...] = jnp.zeros(acc_sc.shape, jnp.float32)

        def step(g, masked):
            for hh in range(heads):
                sl = slice(hh * HDIM, (hh + 1) * HDIM)
                qh = q_ref[:, sl]
                kh = k_ref[g, sl, :]
                vh = v_ref[g, :, sl]
                s = jnp.dot(qh, kh, preferred_element_type=jnp.float32) * scale
                if masked:
                    row = lax.broadcasted_iota(jnp.int32, s.shape, 0)
                    col = lax.broadcasted_iota(jnp.int32, s.shape, 1)
                    allowed = col <= row
                    s = jnp.where(allowed, s, -1e30)
                m_prev = m_sc[hh]
                m_new = jnp.maximum(m_prev, jnp.max(s, axis=1, keepdims=True))
                if s.shape[1] % HDIM == 0:
                    wide = jnp.concatenate([m_new] * (s.shape[1] // HDIM), axis=1)
                else:
                    wide = m_new[:, :1]
                p = jnp.exp(s - wide)
                if masked:
                    p = jnp.where(allowed, p, 0.0)
                fade = jnp.exp(m_prev - m_new)
                l_sc[hh] = l_sc[hh] * fade + jnp.sum(p, axis=1, keepdims=True)
                acc_sc[hh] = acc_sc[hh] * fade + jnp.dot(
                    p.astype(jnp.bfloat16), vh, preferred_element_type=jnp.float32
                )
                m_sc[hh] = m_new

        for g in range(group):
            here = j * group + g

            @pl.when(here < c)
            def _():
                step(g, False)

            @pl.when(here == c)
            def _():
                step(g, True)

        @pl.when(j == nb - 1)
        def _():
            for hh in range(heads):
                sl = slice(hh * HDIM, (hh + 1) * HDIM)
                o_ref[:, sl] = (acc_sc[hh] / l_sc[hh]).astype(o_ref.dtype)

    grid_spec = pltpu.PrefetchScalarGridSpec(
        num_scalar_prefetch=1,
        grid=(nb,),
        in_specs=[
            pl.BlockSpec((rows, width), lambda j, c: (0, 0)),
            pl.BlockSpec((group, width, rows), lambda j, c: (jnp.minimum(j, c[0] // group), 0, 0)),
            pl.BlockSpec((group, rows, width), lambda j, c: (jnp.minimum(j, c[0] // group), 0, part)),
        ],
        out_specs=pl.BlockSpec((rows, width), lambda j, c: (0, 0)),
        scratch_shapes=[
            pltpu.VMEM((heads, rows, HDIM), jnp.float32),
            pltpu.VMEM((heads, rows, HDIM), jnp.float32),
            pltpu.VMEM((heads, rows, HDIM), jnp.float32),
        ],
    )
    return pl.pallas_call(
        kernel,
        grid_spec=grid_spec,
        out_shape=jax.ShapeDtypeStruct((rows, width), jnp.bfloat16),
        compiler_params=pltpu.CompilerParams(dimension_semantics=("arbitrary",)),
    )(jnp.reshape(shard, (1,)).astype(jnp.int32), q_glob, kt_all, v_all)


SWAP = [(0, 1), (1, 0)]


def exchange_heads(stacked, groups):
    if groups != 2:
        return lax.all_to_all(stacked, "hg", split_axis=2, concat_axis=0, tiled=True)[:, :, 0]
    first = lax.axis_index("hg") == 0
    own = jnp.where(first, stacked[:, :, 0], stacked[:, :, 1])
    got = lax.ppermute(jnp.where(first, stacked[:, :, 1], stacked[:, :, 0]), "hg", SWAP)
    return jnp.where(
        first, jnp.concatenate([own, got], axis=0), jnp.concatenate([got, own], axis=0)
    )


def project_out(parts, out_weight, w_other, groups):
    if groups != 2:
        return lax.psum_scatter(
            jnp.dot(
                jnp.concatenate(parts, axis=1), out_weight, preferred_element_type=jnp.float32
            ).astype(jnp.bfloat16),
            "hg",
            scatter_dimension=0,
            tiled=True,
        )
    half = parts[0].shape[0] // 2
    first = lax.axis_index("hg") == 0
    got = [
        lax.ppermute(jnp.where(first, a[half:], a[:half]), "hg", SWAP) for a in parts
    ]
    mine = jnp.concatenate([jnp.where(first, a[:half], a[half:]) for a in parts], axis=1)
    total = jnp.dot(mine, out_weight, preferred_element_type=jnp.float32)
    for a, w in zip(got, w_other):
        total = total + jnp.dot(a, w, preferred_element_type=jnp.float32)
    return total.astype(jnp.bfloat16)


def local(queries, keys, values, reflect_ids, reflect_bank, out_weight):
    groups = lax.axis_size("hg")
    heads = reflect_ids.shape[1]
    width = heads * HDIM
    stacked = jnp.stack([queries, keys, values], axis=1).reshape(
        queries.shape[0], 3, groups, width
    )
    swapped, reflect_ids = lax.optimization_barrier((exchange_heads(stacked, groups), reflect_ids))
    rows = swapped.shape[0]
    q_local = swapped[:, 0]
    k_local = swapped[:, 1]
    v_local = swapped[:, 2]
    v_all = lax.all_gather(v_local, "ctx", axis=0, tiled=False)

    nblocks = rows // BLK
    bank = reflect_bank.shape[0]
    table = reflect_bank.reshape(bank, heads, HDIM).transpose(1, 0, 2)
    onehot = (
        reflect_ids.T[:, :, None] == lax.broadcasted_iota(jnp.int32, (1, 1, bank), 2)
    ).astype(reflect_bank.dtype)
    chosen = jnp.einsum(
        "htb,hbd->htd", onehot, table, preferred_element_type=jnp.float32
    )
    vectors = chosen * lax.rsqrt(jnp.sum(chosen * chosen, axis=-1, keepdims=True) + 1e-06)
    blocks = vectors.reshape(heads, nblocks, BLK, HDIM)
    gram = jnp.einsum("hnkd,hnjd->hnkj", blocks, blocks, precision=HP)
    coupling = 2.0 * jnp.triu(gram, 1)
    tri_factor = 2.0 * invert_unit_upper(coupling)
    spread = jnp.einsum("hnkj,hnje->hnke", tri_factor, blocks, precision=HP)
    eye_d = jnp.eye(HDIM, dtype=jnp.float32)
    block_mats = eye_d - jnp.einsum("hnkd,hnke->hnde", blocks, spread, precision=HP)
    lower_mask = jnp.tril(jnp.ones((BLK, BLK), dtype=jnp.bool_))

    inner_prefix, shard_prod = exclusive_blocks(block_mats)
    parts = 2 if heads % 2 == 0 else 1
    pw = width // parts
    w_other = [None] * parts
    if groups == 2:
        w_other = [
            lax.ppermute(out_weight[p * pw : (p + 1) * pw], "hg", SWAP) for p in range(parts)
        ]
    earlier_prod, v_all, w_other[0] = lax.optimization_barrier(
        (exclusive_shards(shard_prod, "ctx"), v_all, w_other[0])
    )

    def in_shard(matrix):
        split = matrix.astype(jnp.float32).reshape(nblocks, BLK, heads, HDIM).transpose(2, 0, 1, 3)
        proj = jnp.einsum("hnid,hnkd->hnik", split, blocks, precision=HP)
        proj = jnp.where(lower_mask, proj, 0.0)
        coef = jnp.einsum("hnik,hnrk->hnir", proj, tri_factor, precision=HP)
        inblock = split - jnp.einsum("hnir,hnrd->hnid", coef, blocks, precision=HP)
        moved = jnp.einsum("hnid,hned->hnie", inblock, inner_prefix, precision=HP)
        return moved.reshape(heads, rows, HDIM)

    kt_glob = jnp.einsum(
        "hie,hfe->hfi", in_shard(k_local), earlier_prod, precision=HP
    ).reshape(width, rows).astype(jnp.bfloat16)
    if parts > 1:
        kt_glob, w_other[1:] = lax.optimization_barrier((kt_glob, w_other[1:]))
    kt_parts = [
        lax.all_gather(kt_glob[p * pw : (p + 1) * pw], "ctx", axis=0, tiled=False)
        for p in range(parts)
    ]
    q_glob = (
        jnp.einsum("hie,hfe->hif", in_shard(q_local), earlier_prod, precision=HP)
        .transpose(1, 0, 2)
        .reshape(rows, width)
        .astype(jnp.bfloat16)
    )
    shard = lax.axis_index("ctx")
    attn = [
        flash_attend(q_glob[:, p * pw : (p + 1) * pw], kt_parts[p], v_all, p, shard, heads // parts)
        for p in range(parts)
    ]
    return project_out(attn, out_weight, w_other, groups)


def solution(mesh):
    placed = (
        P(("ctx", "hg"), None),
        P(("ctx", "hg"), None),
        P(("ctx", "hg"), None),
        P("ctx", "hg"),
        P(None, "hg"),
        P("hg", None),
    )
    return jax.shard_map(
        local, mesh=mesh, in_specs=placed, out_specs=P(("ctx", "hg"), None), check_vma=False
    )
```

```python
import math

import jax
import jax.numpy as jnp
from jax import lax
from jax.experimental import pallas as pl
from jax.experimental.pallas import tpu as pltpu
from jax.sharding import PartitionSpec as P

HDIM = 128
BLK = 32
GROUP = 1
HP = lax.Precision.HIGHEST


def mm(a, b):
    return jnp.einsum("...ij,...jk->...ik", a, b, precision=HP)


def invert_unit_upper(strict):
    eye_blk = jnp.eye(strict.shape[-1], dtype=jnp.float32)
    result = eye_blk - strict
    power = strict
    steps = strict.shape[-1].bit_length()
    for level in range(steps):
        power = mm(power, power)
        result = mm(result, eye_blk + power)
    return result


def exclusive_blocks(mats):
    heads, n, d, _ = mats.shape
    eye = jnp.broadcast_to(jnp.eye(d, dtype=jnp.float32), (heads, 1, d, d))
    acc = jnp.concatenate([eye, mats[:, :-1]], axis=1)
    shift = 1
    while shift < n:
        earlier = jnp.concatenate(
            [jnp.broadcast_to(eye, (heads, shift, d, d)), acc[:, : n - shift]], axis=1
        )
        acc = mm(earlier, acc)
        shift *= 2
    return acc, mm(acc[:, -1], mats[:, -1])


def exclusive_shards(mat, axis):
    length, here = lax.axis_size(axis), lax.axis_index(axis)
    eye = jnp.broadcast_to(jnp.eye(mat.shape[-1], dtype=jnp.float32), mat.shape)
    if length == 1:
        return eye
    acc = lax.ppermute(mat, axis, [(i, i + 1) for i in range(length - 1)])
    acc = jnp.where(here >= 1, acc, eye)
    shift = 1
    while shift < length:
        earlier = lax.ppermute(acc, axis, [(i, i + shift) for i in range(length - shift)])
        acc = jnp.where(here >= shift, mm(earlier, acc), acc)
        shift *= 2
    return acc


def flash_attend(q_glob, kt_all, v_all, part, shard, heads, group=GROUP):
    rows, width = q_glob.shape
    nk = kt_all.shape[0]
    while nk % group:
        group //= 2
    nb = nk // group
    scale = 1.0 / math.sqrt(HDIM)

    def kernel(c_ref, q_ref, k_ref, v_ref, o_ref, m_sc, l_sc, acc_sc):
        j = pl.program_id(0)
        c = c_ref[0]

        @pl.when(j == 0)
        def _():
            m_sc[...] = jnp.full(m_sc.shape, -1e30, jnp.float32)
            l_sc[...] = jnp.zeros(l_sc.shape, jnp.float32)
            acc_sc[...] = jnp.zeros(acc_sc.shape, jnp.float32)

        def step(g, masked):
            for hh in range(heads):
                sl = slice(hh * HDIM, (hh + 1) * HDIM)
                qh = q_ref[:, sl]
                kh = k_ref[g, sl, :]
                vh = v_ref[g, :, sl]
                s = jnp.dot(qh, kh, preferred_element_type=jnp.float32) * scale
                if masked:
                    row = lax.broadcasted_iota(jnp.int32, s.shape, 0)
                    col = lax.broadcasted_iota(jnp.int32, s.shape, 1)
                    allowed = col <= row
                    s = jnp.where(allowed, s, -1e30)
                m_prev = m_sc[hh]
                m_new = jnp.maximum(m_prev, jnp.max(s, axis=1, keepdims=True))
                if s.shape[1] % HDIM == 0:
                    wide = jnp.concatenate([m_new] * (s.shape[1] // HDIM), axis=1)
                else:
                    wide = m_new[:, :1]
                p = jnp.exp(s - wide)
                if masked:
                    p = jnp.where(allowed, p, 0.0)
                fade = jnp.exp(m_prev - m_new)
                l_sc[hh] = l_sc[hh] * fade + jnp.sum(p, axis=1, keepdims=True)
                acc_sc[hh] = acc_sc[hh] * fade + jnp.dot(
                    p.astype(jnp.bfloat16), vh, preferred_element_type=jnp.float32
                )
                m_sc[hh] = m_new

        for g in range(group):
            here = j * group + g

            @pl.when(here < c)
            def _():
                step(g, False)

            @pl.when(here == c)
            def _():
                step(g, True)

        @pl.when(j == nb - 1)
        def _():
            for hh in range(heads):
                sl = slice(hh * HDIM, (hh + 1) * HDIM)
                o_ref[:, sl] = (acc_sc[hh] / l_sc[hh]).astype(o_ref.dtype)

    grid_spec = pltpu.PrefetchScalarGridSpec(
        num_scalar_prefetch=1,
        grid=(nb,),
        in_specs=[
            pl.BlockSpec((rows, width), lambda j, c: (0, 0)),
            pl.BlockSpec((group, width, rows), lambda j, c: (jnp.minimum(j, c[0] // group), 0, 0)),
            pl.BlockSpec((group, rows, width), lambda j, c: (jnp.minimum(j, c[0] // group), 0, part)),
        ],
        out_specs=pl.BlockSpec((rows, width), lambda j, c: (0, 0)),
        scratch_shapes=[
            pltpu.VMEM((heads, rows, HDIM), jnp.float32),
            pltpu.VMEM((heads, rows, HDIM), jnp.float32),
            pltpu.VMEM((heads, rows, HDIM), jnp.float32),
        ],
    )
    return pl.pallas_call(
        kernel,
        grid_spec=grid_spec,
        out_shape=jax.ShapeDtypeStruct((rows, width), jnp.bfloat16),
        compiler_params=pltpu.CompilerParams(dimension_semantics=("arbitrary",)),
    )(jnp.reshape(shard, (1,)).astype(jnp.int32), q_glob, kt_all, v_all)


SWAP = [(0, 1), (1, 0)]


def exchange_heads(x, groups, width):
    if groups != 2:
        split = x.reshape(x.shape[0], groups, width)
        return lax.all_to_all(split, "hg", split_axis=1, concat_axis=0, tiled=True)[:, 0]
    first = lax.axis_index("hg") == 0
    own = jnp.where(first, x[:, :width], x[:, width:])
    got = lax.ppermute(jnp.where(first, x[:, width:], x[:, :width]), "hg", SWAP)
    return jnp.where(
        first, jnp.concatenate([own, got], axis=0), jnp.concatenate([got, own], axis=0)
    )


def project_out(attn, out_weight, groups):
    if groups != 2:
        return lax.psum_scatter(
            jnp.dot(attn, out_weight, preferred_element_type=jnp.float32).astype(jnp.bfloat16),
            "hg",
            scatter_dimension=0,
            tiled=True,
        )
    half = attn.shape[0] // 2
    first = lax.axis_index("hg") == 0
    theirs = jnp.where(first, attn[half:], attn[:half])
    mine = jnp.where(first, attn[:half], attn[half:])
    sent = jnp.dot(theirs, out_weight, preferred_element_type=jnp.float32).astype(jnp.bfloat16)
    got = lax.ppermute(sent, "hg", SWAP)
    kept = jnp.dot(mine, out_weight, preferred_element_type=jnp.float32)
    return (kept + got.astype(jnp.float32)).astype(jnp.bfloat16)


def local(queries, keys, values, reflect_ids, reflect_bank, out_weight):
    groups = lax.axis_size("hg")
    heads = reflect_ids.shape[1]
    width = heads * HDIM
    q_local, k_local, v_local = (exchange_heads(x, groups, width) for x in (queries, keys, values))
    rows = q_local.shape[0]
    v_all = lax.all_gather(v_local, "ctx", axis=0, tiled=False)

    nblocks = rows // BLK
    bank = reflect_bank.shape[0]
    table = reflect_bank.reshape(bank, heads, HDIM).transpose(1, 0, 2)
    onehot = (
        reflect_ids.T[:, :, None] == lax.broadcasted_iota(jnp.int32, (1, 1, bank), 2)
    ).astype(reflect_bank.dtype)
    chosen = jnp.einsum(
        "htb,hbd->htd", onehot, table, preferred_element_type=jnp.float32
    )
    vectors = chosen * lax.rsqrt(jnp.sum(chosen * chosen, axis=-1, keepdims=True) + 1e-06)
    blocks = vectors.reshape(heads, nblocks, BLK, HDIM)
    gram = jnp.einsum("hnkd,hnjd->hnkj", blocks, blocks, precision=HP)
    gram, q_local, k_local, v_local = lax.optimization_barrier((gram, q_local, k_local, v_local))
    coupling = 2.0 * jnp.triu(gram, 1)
    tri_factor = 2.0 * invert_unit_upper(coupling)
    spread = jnp.einsum("hnkj,hnje->hnke", tri_factor, blocks, precision=HP)
    eye_d = jnp.eye(HDIM, dtype=jnp.float32)
    block_mats = eye_d - jnp.einsum("hnkd,hnke->hnde", blocks, spread, precision=HP)
    lower_mask = jnp.tril(jnp.ones((BLK, BLK), dtype=jnp.bool_))

    inner_prefix, shard_prod = exclusive_blocks(block_mats)
    earlier_prod, v_all = lax.optimization_barrier((exclusive_shards(shard_prod, "ctx"), v_all))

    def in_shard(matrix):
        split = matrix.astype(jnp.float32).reshape(nblocks, BLK, heads, HDIM).transpose(2, 0, 1, 3)
        proj = jnp.einsum("hnid,hnkd->hnik", split, blocks, precision=HP)
        proj = jnp.where(lower_mask, proj, 0.0)
        coef = jnp.einsum("hnik,hnrk->hnir", proj, tri_factor, precision=HP)
        inblock = split - jnp.einsum("hnir,hnrd->hnid", coef, blocks, precision=HP)
        moved = jnp.einsum("hnid,hned->hnie", inblock, inner_prefix, precision=HP)
        return moved.reshape(heads, rows, HDIM)

    kt_glob = jnp.einsum(
        "hie,hfe->hfi", in_shard(k_local), earlier_prod, precision=HP
    ).reshape(width, rows).astype(jnp.bfloat16)
    parts = 2 if heads % 2 == 0 else 1
    pw = width // parts
    kt_parts = [
        lax.all_gather(kt_glob[p * pw : (p + 1) * pw], "ctx", axis=0, tiled=False)
        for p in range(parts)
    ]
    q_glob = (
        jnp.einsum("hie,hfe->hif", in_shard(q_local), earlier_prod, precision=HP)
        .transpose(1, 0, 2)
        .reshape(rows, width)
        .astype(jnp.bfloat16)
    )
    shard = lax.axis_index("ctx")
    attn = jnp.concatenate(
        [
            flash_attend(q_glob[:, p * pw : (p + 1) * pw], kt_parts[p], v_all, p, shard, heads // parts)
            for p in range(parts)
        ],
        axis=1,
    )
    return project_out(attn, out_weight, groups)


def solution(mesh):
    placed = (
        P(("ctx", "hg"), None),
        P(("ctx", "hg"), None),
        P(("ctx", "hg"), None),
        P("ctx", "hg"),
        P(None, "hg"),
        P("hg", None),
    )
    return jax.shard_map(
        local, mesh=mesh, in_specs=placed, out_specs=P(("ctx", "hg"), None), check_vma=False
    )
```

```python
import math

import jax
import jax.numpy as jnp
from jax import lax
from jax.experimental import pallas as pl
from jax.experimental.pallas import tpu as pltpu
from jax.sharding import PartitionSpec as P

HDIM = 128
BLK = 32
GROUP = 1
HP = lax.Precision.HIGHEST


def mm(a, b):
    return jnp.einsum("...ij,...jk->...ik", a, b, precision=HP)


def invert_unit_upper(strict):
    eye_blk = jnp.eye(strict.shape[-1], dtype=jnp.float32)
    result = eye_blk - strict
    power = strict
    steps = strict.shape[-1].bit_length()
    for level in range(steps):
        power = mm(power, power)
        result = mm(result, eye_blk + power)
    return result


def exclusive_blocks(mats):
    heads, n, d, _ = mats.shape
    eye = jnp.broadcast_to(jnp.eye(d, dtype=jnp.float32), (heads, 1, d, d))
    acc = jnp.concatenate([eye, mats[:, :-1]], axis=1)
    shift = 1
    while shift < n:
        earlier = jnp.concatenate(
            [jnp.broadcast_to(eye, (heads, shift, d, d)), acc[:, : n - shift]], axis=1
        )
        acc = mm(earlier, acc)
        shift *= 2
    return acc, mm(acc[:, -1], mats[:, -1])


def exclusive_shards(mat, axis):
    length, here = lax.axis_size(axis), lax.axis_index(axis)
    eye = jnp.broadcast_to(jnp.eye(mat.shape[-1], dtype=jnp.float32), mat.shape)
    sizes = []
    rest = length
    for size in (2, 2):
        if rest % size == 0 and rest > size:
            sizes.append(size)
            rest //= size
    sizes.append(rest)
    block, before, stride = mat, eye, 1
    for level, size in enumerate(sizes):
        if size == 1:
            continue
        pos = (here // stride) % size
        last = level == len(sizes) - 1
        got = {}
        for dist in range(1, size):
            forward = [
                (i, i + dist * stride) for i in range(length) if (i // stride) % size + dist < size
            ]
            got[dist] = lax.ppermute(block, axis, forward)
            if not last:
                got[-dist] = lax.ppermute(
                    block, axis, [(b, a) for a, b in forward]
                )
        lead = eye
        for dist in range(size - 1, 0, -1):
            lead = mm(lead, jnp.where(pos >= dist, got[dist], eye))
        before = mm(lead, before)
        if not last:
            tail = block
            for dist in range(1, size):
                tail = mm(tail, jnp.where(pos + dist < size, got[-dist], eye))
            block = mm(lead, tail)
        stride *= size
    return before


def flash_attend(q_glob, kt_all, v_all, part, shard, heads, group=GROUP):
    rows, width = q_glob.shape
    nk = kt_all.shape[0]
    while nk % group:
        group //= 2
    nb = nk // group
    scale = 1.0 / math.sqrt(HDIM)

    def kernel(c_ref, q_ref, k_ref, v_ref, o_ref, m_sc, l_sc, acc_sc):
        j = pl.program_id(0)
        c = c_ref[0]

        @pl.when(j == 0)
        def _():
            m_sc[...] = jnp.full(m_sc.shape, -1e30, jnp.float32)
            l_sc[...] = jnp.zeros(l_sc.shape, jnp.float32)
            acc_sc[...] = jnp.zeros(acc_sc.shape, jnp.float32)

        def step(g, masked):
            for hh in range(heads):
                sl = slice(hh * HDIM, (hh + 1) * HDIM)
                qh = q_ref[:, sl]
                kh = k_ref[g, sl, :]
                vh = v_ref[g, :, sl]
                s = jnp.dot(qh, kh, preferred_element_type=jnp.float32) * scale
                if masked:
                    row = lax.broadcasted_iota(jnp.int32, s.shape, 0)
                    col = lax.broadcasted_iota(jnp.int32, s.shape, 1)
                    allowed = col <= row
                    s = jnp.where(allowed, s, -1e30)
                m_prev = m_sc[hh]
                m_new = jnp.maximum(m_prev, jnp.max(s, axis=1, keepdims=True))
                if s.shape[1] % HDIM == 0:
                    wide = jnp.concatenate([m_new] * (s.shape[1] // HDIM), axis=1)
                else:
                    wide = m_new[:, :1]
                p = jnp.exp(s - wide)
                if masked:
                    p = jnp.where(allowed, p, 0.0)
                fade = jnp.exp(m_prev - m_new)
                l_sc[hh] = l_sc[hh] * fade + jnp.sum(p, axis=1, keepdims=True)
                acc_sc[hh] = acc_sc[hh] * fade + jnp.dot(
                    p.astype(jnp.bfloat16), vh, preferred_element_type=jnp.float32
                )
                m_sc[hh] = m_new

        for g in range(group):
            here = j * group + g

            @pl.when(here < c)
            def _():
                step(g, False)

            @pl.when(here == c)
            def _():
                step(g, True)

        @pl.when(j == nb - 1)
        def _():
            for hh in range(heads):
                sl = slice(hh * HDIM, (hh + 1) * HDIM)
                o_ref[:, sl] = (acc_sc[hh] / l_sc[hh]).astype(o_ref.dtype)

    grid_spec = pltpu.PrefetchScalarGridSpec(
        num_scalar_prefetch=1,
        grid=(nb,),
        in_specs=[
            pl.BlockSpec((rows, width), lambda j, c: (0, 0)),
            pl.BlockSpec((group, width, rows), lambda j, c: (jnp.minimum(j, c[0] // group), 0, 0)),
            pl.BlockSpec((group, rows, width), lambda j, c: (jnp.minimum(j, c[0] // group), 0, part)),
        ],
        out_specs=pl.BlockSpec((rows, width), lambda j, c: (0, 0)),
        scratch_shapes=[
            pltpu.VMEM((heads, rows, HDIM), jnp.float32),
            pltpu.VMEM((heads, rows, HDIM), jnp.float32),
            pltpu.VMEM((heads, rows, HDIM), jnp.float32),
        ],
    )
    return pl.pallas_call(
        kernel,
        grid_spec=grid_spec,
        out_shape=jax.ShapeDtypeStruct((rows, width), jnp.bfloat16),
        compiler_params=pltpu.CompilerParams(dimension_semantics=("arbitrary",)),
    )(jnp.reshape(shard, (1,)).astype(jnp.int32), q_glob, kt_all, v_all)


SWAP = [(0, 1), (1, 0)]


def exchange_heads(x, groups, width):
    if groups != 2:
        split = x.reshape(x.shape[0], groups, width)
        return lax.all_to_all(split, "hg", split_axis=1, concat_axis=0, tiled=True)[:, 0]
    first = lax.axis_index("hg") == 0
    own = jnp.where(first, x[:, :width], x[:, width:])
    got = lax.ppermute(jnp.where(first, x[:, width:], x[:, :width]), "hg", SWAP)
    return jnp.where(
        first, jnp.concatenate([own, got], axis=0), jnp.concatenate([got, own], axis=0)
    )


def project_out(attn, out_weight, groups):
    if groups != 2:
        return lax.psum_scatter(
            jnp.dot(attn, out_weight, preferred_element_type=jnp.float32).astype(jnp.bfloat16),
            "hg",
            scatter_dimension=0,
            tiled=True,
        )
    half = attn.shape[0] // 2
    first = lax.axis_index("hg") == 0
    theirs = jnp.where(first, attn[half:], attn[:half])
    mine = jnp.where(first, attn[:half], attn[half:])
    sent = jnp.dot(theirs, out_weight, preferred_element_type=jnp.float32).astype(jnp.bfloat16)
    got = lax.ppermute(sent, "hg", SWAP)
    kept = jnp.dot(mine, out_weight, preferred_element_type=jnp.float32)
    return (kept + got.astype(jnp.float32)).astype(jnp.bfloat16)


def local(queries, keys, values, reflect_ids, reflect_bank, out_weight):
    groups = lax.axis_size("hg")
    heads = reflect_ids.shape[1]
    width = heads * HDIM
    q_local, k_local, v_local = (exchange_heads(x, groups, width) for x in (queries, keys, values))
    rows = q_local.shape[0]
    v_all = lax.all_gather(v_local, "ctx", axis=0, tiled=False)

    nblocks = rows // BLK
    bank = reflect_bank.shape[0]
    table = reflect_bank.reshape(bank, heads, HDIM).transpose(1, 0, 2)
    onehot = (
        reflect_ids.T[:, :, None] == lax.broadcasted_iota(jnp.int32, (1, 1, bank), 2)
    ).astype(reflect_bank.dtype)
    chosen = jnp.einsum(
        "htb,hbd->htd", onehot, table, preferred_element_type=jnp.float32
    )
    vectors = chosen * lax.rsqrt(jnp.sum(chosen * chosen, axis=-1, keepdims=True) + 1e-06)
    blocks = vectors.reshape(heads, nblocks, BLK, HDIM)
    gram = jnp.einsum("hnkd,hnjd->hnkj", blocks, blocks, precision=HP)
    gram, q_local, k_local, v_local = lax.optimization_barrier((gram, q_local, k_local, v_local))
    coupling = 2.0 * jnp.triu(gram, 1)
    tri_factor = 2.0 * invert_unit_upper(coupling)
    spread = jnp.einsum("hnkj,hnje->hnke", tri_factor, blocks, precision=HP)
    eye_d = jnp.eye(HDIM, dtype=jnp.float32)
    block_mats = eye_d - jnp.einsum("hnkd,hnke->hnde", blocks, spread, precision=HP)
    lower_mask = jnp.tril(jnp.ones((BLK, BLK), dtype=jnp.bool_))

    inner_prefix, shard_prod = exclusive_blocks(block_mats)
    earlier_prod, v_all = lax.optimization_barrier((exclusive_shards(shard_prod, "ctx"), v_all))

    def in_shard(matrix):
        split = matrix.astype(jnp.float32).reshape(nblocks, BLK, heads, HDIM).transpose(2, 0, 1, 3)
        proj = jnp.einsum("hnid,hnkd->hnik", split, blocks, precision=HP)
        proj = jnp.where(lower_mask, proj, 0.0)
        coef = jnp.einsum("hnik,hnrk->hnir", proj, tri_factor, precision=HP)
        inblock = split - jnp.einsum("hnir,hnrd->hnid", coef, blocks, precision=HP)
        moved = jnp.einsum("hnid,hned->hnie", inblock, inner_prefix, precision=HP)
        return moved.reshape(heads, rows, HDIM)

    kt_glob = jnp.einsum(
        "hie,hfe->hfi", in_shard(k_local), earlier_prod, precision=HP
    ).reshape(width, rows).astype(jnp.bfloat16)
    parts = 2 if heads % 2 == 0 else 1
    pw = width // parts
    kt_parts = [
        lax.all_gather(kt_glob[p * pw : (p + 1) * pw], "ctx", axis=0, tiled=False)
        for p in range(parts)
    ]
    q_glob = (
        jnp.einsum("hie,hfe->hif", in_shard(q_local), earlier_prod, precision=HP)
        .transpose(1, 0, 2)
        .reshape(rows, width)
        .astype(jnp.bfloat16)
    )
    shard = lax.axis_index("ctx")
    attn = jnp.concatenate(
        [
            flash_attend(q_glob[:, p * pw : (p + 1) * pw], kt_parts[p], v_all, p, shard, heads // parts)
            for p in range(parts)
        ],
        axis=1,
    )
    return project_out(attn, out_weight, groups)


def solution(mesh):
    placed = (
        P(("ctx", "hg"), None),
        P(("ctx", "hg"), None),
        P(("ctx", "hg"), None),
        P("ctx", "hg"),
        P(None, "hg"),
        P("hg", None),
    )
    return jax.shard_map(
        local, mesh=mesh, in_specs=placed, out_specs=P(("ctx", "hg"), None), check_vma=False
    )
```

```python
import math

import jax
import jax.numpy as jnp
from jax import lax
from jax.experimental import pallas as pl
from jax.experimental.pallas import tpu as pltpu
from jax.sharding import PartitionSpec as P

HDIM = 128
BLK = 32
GROUP = 1
HP = lax.Precision.HIGHEST


def mm(a, b):
    return jnp.einsum("...ij,...jk->...ik", a, b, precision=HP)


def invert_unit_upper(strict):
    eye_blk = jnp.eye(strict.shape[-1], dtype=jnp.float32)
    result = eye_blk - strict
    power = strict
    steps = strict.shape[-1].bit_length()
    for level in range(steps):
        power = mm(power, power)
        result = mm(result, eye_blk + power)
    return result


def exclusive_blocks(mats):
    heads, n, d, _ = mats.shape
    eye = jnp.broadcast_to(jnp.eye(d, dtype=jnp.float32), (heads, 1, d, d))
    acc = jnp.concatenate([eye, mats[:, :-1]], axis=1)
    shift = 1
    while shift < n:
        earlier = jnp.concatenate(
            [jnp.broadcast_to(eye, (heads, shift, d, d)), acc[:, : n - shift]], axis=1
        )
        acc = mm(earlier, acc)
        shift *= 2
    return acc, mm(acc[:, -1], mats[:, -1])


def exclusive_shards(mat, axis):
    length, here = lax.axis_size(axis), lax.axis_index(axis)
    eye = jnp.broadcast_to(jnp.eye(mat.shape[-1], dtype=jnp.float32), mat.shape)
    sizes = []
    rest = length
    for size in (2, 2):
        if rest % size == 0 and rest > size:
            sizes.append(size)
            rest //= size
    sizes.append(rest)
    block, before, stride = mat, eye, 1
    for level, size in enumerate(sizes):
        if size == 1:
            continue
        pos = (here // stride) % size
        last = level == len(sizes) - 1
        got = {}
        for dist in range(1, size):
            forward = [
                (i, i + dist * stride) for i in range(length) if (i // stride) % size + dist < size
            ]
            got[dist] = lax.ppermute(block, axis, forward)
            if not last:
                got[-dist] = lax.ppermute(
                    block, axis, [(b, a) for a, b in forward]
                )
        lead = eye
        for dist in range(size - 1, 0, -1):
            lead = mm(lead, jnp.where(pos >= dist, got[dist], eye))
        before = mm(lead, before)
        if not last:
            tail = block
            for dist in range(1, size):
                tail = mm(tail, jnp.where(pos + dist < size, got[-dist], eye))
            block = mm(lead, tail)
        stride *= size
    return before


def flash_attend(q_glob, kt_all, v_all, part, shard, heads, group=GROUP):
    rows, width = q_glob.shape
    nk = kt_all.shape[0]
    while nk % group:
        group //= 2
    nb = nk // group
    scale = 1.0 / math.sqrt(HDIM)

    def kernel(c_ref, q_ref, k_ref, v_ref, o_ref, m_sc, l_sc, acc_sc):
        j = pl.program_id(0)
        c = c_ref[0]

        @pl.when(j == 0)
        def _():
            m_sc[...] = jnp.full(m_sc.shape, -1e30, jnp.float32)
            l_sc[...] = jnp.zeros(l_sc.shape, jnp.float32)
            acc_sc[...] = jnp.zeros(acc_sc.shape, jnp.float32)

        def step(g, masked):
            for hh in range(heads):
                sl = slice(hh * HDIM, (hh + 1) * HDIM)
                qh = q_ref[:, sl]
                kh = k_ref[g, sl, :]
                vh = v_ref[g, :, sl]
                s = jnp.dot(qh, kh, preferred_element_type=jnp.float32) * scale
                if masked:
                    row = lax.broadcasted_iota(jnp.int32, s.shape, 0)
                    col = lax.broadcasted_iota(jnp.int32, s.shape, 1)
                    allowed = col <= row
                    s = jnp.where(allowed, s, -1e30)
                m_prev = m_sc[hh]
                m_new = jnp.maximum(m_prev, jnp.max(s, axis=1, keepdims=True))
                if s.shape[1] % HDIM == 0:
                    wide = jnp.concatenate([m_new] * (s.shape[1] // HDIM), axis=1)
                else:
                    wide = m_new[:, :1]
                p = jnp.exp(s - wide)
                if masked:
                    p = jnp.where(allowed, p, 0.0)
                fade = jnp.exp(m_prev - m_new)
                l_sc[hh] = l_sc[hh] * fade + jnp.sum(p, axis=1, keepdims=True)
                acc_sc[hh] = acc_sc[hh] * fade + jnp.dot(
                    p.astype(jnp.bfloat16), vh, preferred_element_type=jnp.float32
                )
                m_sc[hh] = m_new

        for g in range(group):
            here = j * group + g

            @pl.when(here < c)
            def _():
                step(g, False)

            @pl.when(here == c)
            def _():
                step(g, True)

        @pl.when(j == nb - 1)
        def _():
            for hh in range(heads):
                sl = slice(hh * HDIM, (hh + 1) * HDIM)
                o_ref[:, sl] = (acc_sc[hh] / l_sc[hh]).astype(o_ref.dtype)

    grid_spec = pltpu.PrefetchScalarGridSpec(
        num_scalar_prefetch=1,
        grid=(nb,),
        in_specs=[
            pl.BlockSpec((rows, width), lambda j, c: (0, 0)),
            pl.BlockSpec((group, width, rows), lambda j, c: (jnp.minimum(j, c[0] // group), 0, 0)),
            pl.BlockSpec((group, rows, width), lambda j, c: (jnp.minimum(j, c[0] // group), 0, part)),
        ],
        out_specs=pl.BlockSpec((rows, width), lambda j, c: (0, 0)),
        scratch_shapes=[
            pltpu.VMEM((heads, rows, HDIM), jnp.float32),
            pltpu.VMEM((heads, rows, HDIM), jnp.float32),
            pltpu.VMEM((heads, rows, HDIM), jnp.float32),
        ],
    )
    return pl.pallas_call(
        kernel,
        grid_spec=grid_spec,
        out_shape=jax.ShapeDtypeStruct((rows, width), jnp.bfloat16),
        compiler_params=pltpu.CompilerParams(dimension_semantics=("arbitrary",)),
    )(jnp.reshape(shard, (1,)).astype(jnp.int32), q_glob, kt_all, v_all)


SWAP = [(0, 1), (1, 0)]


def exchange_heads(x, groups, width):
    if groups != 2:
        split = x.reshape(x.shape[0], groups, width)
        return lax.all_to_all(split, "hg", split_axis=1, concat_axis=0, tiled=True)[:, 0]
    first = lax.axis_index("hg") == 0
    own = jnp.where(first, x[:, :width], x[:, width:])
    got = lax.ppermute(jnp.where(first, x[:, width:], x[:, :width]), "hg", SWAP)
    return jnp.where(
        first, jnp.concatenate([own, got], axis=0), jnp.concatenate([got, own], axis=0)
    )


def project_out(attn, out_weight, groups):
    if groups != 2:
        return lax.psum_scatter(
            jnp.dot(attn, out_weight, preferred_element_type=jnp.float32).astype(jnp.bfloat16),
            "hg",
            scatter_dimension=0,
            tiled=True,
        )
    half = attn.shape[0] // 2
    first = lax.axis_index("hg") == 0
    theirs = jnp.where(first, attn[half:], attn[:half])
    mine = jnp.where(first, attn[:half], attn[half:])
    sent = jnp.dot(theirs, out_weight, preferred_element_type=jnp.float32).astype(jnp.bfloat16)
    cols = sent.shape[1] // 2
    got = jnp.concatenate(
        [lax.ppermute(sent[:, :cols], "hg", SWAP), lax.ppermute(sent[:, cols:], "hg", SWAP)],
        axis=1,
    )
    kept = jnp.dot(mine, out_weight, preferred_element_type=jnp.float32)
    return (kept + got.astype(jnp.float32)).astype(jnp.bfloat16)


def local(queries, keys, values, reflect_ids, reflect_bank, out_weight):
    groups = lax.axis_size("hg")
    heads = reflect_ids.shape[1]
    width = heads * HDIM
    q_local, k_local, v_local = (exchange_heads(x, groups, width) for x in (queries, keys, values))
    rows = q_local.shape[0]
    v_all = lax.all_gather(v_local, "ctx", axis=0, tiled=False)

    nblocks = rows // BLK
    bank = reflect_bank.shape[0]
    table = reflect_bank.reshape(bank, heads, HDIM).transpose(1, 0, 2)
    onehot = (
        reflect_ids.T[:, :, None] == lax.broadcasted_iota(jnp.int32, (1, 1, bank), 2)
    ).astype(reflect_bank.dtype)
    chosen = jnp.einsum(
        "htb,hbd->htd", onehot, table, preferred_element_type=jnp.float32
    )
    vectors = chosen * lax.rsqrt(jnp.sum(chosen * chosen, axis=-1, keepdims=True) + 1e-06)
    blocks = vectors.reshape(heads, nblocks, BLK, HDIM)
    gram = jnp.einsum("hnkd,hnjd->hnkj", blocks, blocks, precision=HP)
    gram, q_local, k_local, v_local = lax.optimization_barrier((gram, q_local, k_local, v_local))
    coupling = 2.0 * jnp.triu(gram, 1)
    tri_factor = 2.0 * invert_unit_upper(coupling)
    spread = jnp.einsum("hnkj,hnje->hnke", tri_factor, blocks, precision=HP)
    eye_d = jnp.eye(HDIM, dtype=jnp.float32)
    block_mats = eye_d - jnp.einsum("hnkd,hnke->hnde", blocks, spread, precision=HP)
    lower_mask = jnp.tril(jnp.ones((BLK, BLK), dtype=jnp.bool_))

    terms = block_mats
    while terms.shape[1] > 1 and terms.shape[1] % 2 == 0:
        terms = mm(terms[:, 0::2], terms[:, 1::2])
    shard_prod = terms[:, 0]
    for extra in range(1, terms.shape[1]):
        shard_prod = mm(shard_prod, terms[:, extra])
    inner_prefix, _ = exclusive_blocks(block_mats)
    earlier_prod, v_all = lax.optimization_barrier((exclusive_shards(shard_prod, "ctx"), v_all))

    def in_shard(matrix):
        split = matrix.astype(jnp.float32).reshape(nblocks, BLK, heads, HDIM).transpose(2, 0, 1, 3)
        proj = jnp.einsum("hnid,hnkd->hnik", split, blocks, precision=HP)
        proj = jnp.where(lower_mask, proj, 0.0)
        coef = jnp.einsum("hnik,hnrk->hnir", proj, tri_factor, precision=HP)
        inblock = split - jnp.einsum("hnir,hnrd->hnid", coef, blocks, precision=HP)
        moved = jnp.einsum("hnid,hned->hnie", inblock, inner_prefix, precision=HP)
        return moved.reshape(heads, rows, HDIM)

    kt_glob = jnp.einsum(
        "hie,hfe->hfi", in_shard(k_local), earlier_prod, precision=HP
    ).reshape(width, rows).astype(jnp.bfloat16)
    parts = 2 if heads % 2 == 0 else 1
    pw = width // parts
    kt_parts = [
        lax.all_gather(kt_glob[p * pw : (p + 1) * pw], "ctx", axis=0, tiled=False)
        for p in range(parts)
    ]
    q_glob = (
        jnp.einsum("hie,hfe->hif", in_shard(q_local), earlier_prod, precision=HP)
        .transpose(1, 0, 2)
        .reshape(rows, width)
        .astype(jnp.bfloat16)
    )
    shard = lax.axis_index("ctx")
    attn = jnp.concatenate(
        [
            flash_attend(q_glob[:, p * pw : (p + 1) * pw], kt_parts[p], v_all, p, shard, heads // parts)
            for p in range(parts)
        ],
        axis=1,
    )
    return project_out(attn, out_weight, groups)


def solution(mesh):
    placed = (
        P(("ctx", "hg"), None),
        P(("ctx", "hg"), None),
        P(("ctx", "hg"), None),
        P("ctx", "hg"),
        P(None, "hg"),
        P("hg", None),
    )
    return jax.shard_map(
        local, mesh=mesh, in_specs=placed, out_specs=P(("ctx", "hg"), None), check_vma=False
    )
```

```python
import math

import jax
import jax.numpy as jnp
from jax import lax
from jax.experimental import pallas as pl
from jax.experimental.pallas import tpu as pltpu
from jax.sharding import PartitionSpec as P

HDIM = 128
BLK = 32
GROUP = 1
HP = lax.Precision.HIGHEST


def mm(a, b):
    return jnp.einsum("...ij,...jk->...ik", a, b, precision=HP)


def invert_unit_upper(strict):
    eye_blk = jnp.eye(strict.shape[-1], dtype=jnp.float32)
    result = eye_blk - strict
    power = strict
    steps = strict.shape[-1].bit_length()
    for level in range(steps):
        power = mm(power, power)
        result = mm(result, eye_blk + power)
    return result


def exclusive_blocks(mats):
    heads, n, d, _ = mats.shape
    eye = jnp.broadcast_to(jnp.eye(d, dtype=jnp.float32), (heads, 1, d, d))
    acc = jnp.concatenate([eye, mats[:, :-1]], axis=1)
    shift = 1
    while shift < n:
        earlier = jnp.concatenate(
            [jnp.broadcast_to(eye, (heads, shift, d, d)), acc[:, : n - shift]], axis=1
        )
        acc = mm(earlier, acc)
        shift *= 2
    return acc, mm(acc[:, -1], mats[:, -1])


def exclusive_shards(mat, axis):
    length, here = lax.axis_size(axis), lax.axis_index(axis)
    eye = jnp.broadcast_to(jnp.eye(mat.shape[-1], dtype=jnp.float32), mat.shape)
    sizes = []
    rest = length
    for size in (2, 2):
        if rest % size == 0 and rest > size:
            sizes.append(size)
            rest //= size
    sizes.append(rest)
    block, before, stride = mat, eye, 1
    for level, size in enumerate(sizes):
        if size == 1:
            continue
        pos = (here // stride) % size
        last = level == len(sizes) - 1
        got = {}
        for dist in range(1, size):
            forward = [
                (i, i + dist * stride) for i in range(length) if (i // stride) % size + dist < size
            ]
            got[dist] = lax.ppermute(block, axis, forward)
            if not last:
                got[-dist] = lax.ppermute(
                    block, axis, [(b, a) for a, b in forward]
                )
        lead = eye
        for dist in range(size - 1, 0, -1):
            lead = mm(lead, jnp.where(pos >= dist, got[dist], eye))
        before = mm(lead, before)
        if not last:
            tail = block
            for dist in range(1, size):
                tail = mm(tail, jnp.where(pos + dist < size, got[-dist], eye))
            block = mm(lead, tail)
        stride *= size
    return before


def flash_attend(q_glob, kt_all, v_all, part, shard, heads, group=GROUP):
    rows, width = q_glob.shape
    nk = kt_all.shape[0]
    while nk % group:
        group //= 2
    nb = nk // group
    scale = 1.0 / math.sqrt(HDIM)

    def kernel(c_ref, q_ref, k_ref, v_ref, o_ref, m_sc, l_sc, acc_sc):
        j = pl.program_id(0)
        c = c_ref[0]

        @pl.when(j == 0)
        def _():
            m_sc[...] = jnp.full(m_sc.shape, -1e30, jnp.float32)
            l_sc[...] = jnp.zeros(l_sc.shape, jnp.float32)
            acc_sc[...] = jnp.zeros(acc_sc.shape, jnp.float32)

        def step(g, masked):
            for hh in range(heads):
                sl = slice(hh * HDIM, (hh + 1) * HDIM)
                qh = q_ref[:, sl]
                kh = k_ref[g, sl, :]
                vh = v_ref[g, :, sl]
                s = jnp.dot(qh, kh, preferred_element_type=jnp.float32) * scale
                if masked:
                    row = lax.broadcasted_iota(jnp.int32, s.shape, 0)
                    col = lax.broadcasted_iota(jnp.int32, s.shape, 1)
                    allowed = col <= row
                    s = jnp.where(allowed, s, -1e30)
                m_prev = m_sc[hh]
                m_new = jnp.maximum(m_prev, jnp.max(s, axis=1, keepdims=True))
                if s.shape[1] % HDIM == 0:
                    wide = jnp.concatenate([m_new] * (s.shape[1] // HDIM), axis=1)
                else:
                    wide = m_new[:, :1]
                p = jnp.exp(s - wide)
                if masked:
                    p = jnp.where(allowed, p, 0.0)
                fade = jnp.exp(m_prev - m_new)
                l_sc[hh] = l_sc[hh] * fade + jnp.sum(p, axis=1, keepdims=True)
                acc_sc[hh] = acc_sc[hh] * fade + jnp.dot(
                    p.astype(jnp.bfloat16), vh, preferred_element_type=jnp.float32
                )
                m_sc[hh] = m_new

        for g in range(group):
            here = j * group + g

            @pl.when(here < c)
            def _():
                step(g, False)

            @pl.when(here == c)
            def _():
                step(g, True)

        @pl.when(j == nb - 1)
        def _():
            for hh in range(heads):
                sl = slice(hh * HDIM, (hh + 1) * HDIM)
                o_ref[:, sl] = (acc_sc[hh] / l_sc[hh]).astype(o_ref.dtype)

    grid_spec = pltpu.PrefetchScalarGridSpec(
        num_scalar_prefetch=1,
        grid=(nb,),
        in_specs=[
            pl.BlockSpec((rows, width), lambda j, c: (0, 0)),
            pl.BlockSpec((group, width, rows), lambda j, c: (jnp.minimum(j, c[0] // group), 0, 0)),
            pl.BlockSpec((group, rows, width), lambda j, c: (jnp.minimum(j, c[0] // group), 0, part)),
        ],
        out_specs=pl.BlockSpec((rows, width), lambda j, c: (0, 0)),
        scratch_shapes=[
            pltpu.VMEM((heads, rows, HDIM), jnp.float32),
            pltpu.VMEM((heads, rows, HDIM), jnp.float32),
            pltpu.VMEM((heads, rows, HDIM), jnp.float32),
        ],
    )
    return pl.pallas_call(
        kernel,
        grid_spec=grid_spec,
        out_shape=jax.ShapeDtypeStruct((rows, width), jnp.bfloat16),
        compiler_params=pltpu.CompilerParams(dimension_semantics=("arbitrary",)),
    )(jnp.reshape(shard, (1,)).astype(jnp.int32), q_glob, kt_all, v_all)


SWAP = [(0, 1), (1, 0)]


def exchange_heads(x, groups, width):
    if groups != 2:
        split = x.reshape(x.shape[0], groups, width)
        return lax.all_to_all(split, "hg", split_axis=1, concat_axis=0, tiled=True)[:, 0]
    first = lax.axis_index("hg") == 0
    own = jnp.where(first, x[:, :width], x[:, width:])
    got = lax.ppermute(jnp.where(first, x[:, width:], x[:, :width]), "hg", SWAP)
    return jnp.where(
        first, jnp.concatenate([own, got], axis=0), jnp.concatenate([got, own], axis=0)
    )


def project_out(parts, out_weight, w_other, groups):
    if groups != 2:
        return lax.psum_scatter(
            jnp.dot(
                jnp.concatenate(parts, axis=1), out_weight, preferred_element_type=jnp.float32
            ).astype(jnp.bfloat16),
            "hg",
            scatter_dimension=0,
            tiled=True,
        )
    half = parts[0].shape[0] // 2
    first = lax.axis_index("hg") == 0
    got = [
        lax.ppermute(jnp.where(first, a[half:], a[:half]), "hg", SWAP) for a in parts
    ]
    mine = jnp.concatenate([jnp.where(first, a[:half], a[half:]) for a in parts], axis=1)
    total = jnp.dot(mine, out_weight, preferred_element_type=jnp.float32)
    for a, w in zip(got, w_other):
        total = total + jnp.dot(a, w, preferred_element_type=jnp.float32)
    return total.astype(jnp.bfloat16)


def local(queries, keys, values, reflect_ids, reflect_bank, out_weight):
    groups = lax.axis_size("hg")
    heads = reflect_ids.shape[1]
    width = heads * HDIM
    q_local, k_local, v_local = (exchange_heads(x, groups, width) for x in (queries, keys, values))
    rows = q_local.shape[0]
    v_all = lax.all_gather(v_local, "ctx", axis=0, tiled=False)

    nblocks = rows // BLK
    bank = reflect_bank.shape[0]
    table = reflect_bank.reshape(bank, heads, HDIM).transpose(1, 0, 2)
    onehot = (
        reflect_ids.T[:, :, None] == lax.broadcasted_iota(jnp.int32, (1, 1, bank), 2)
    ).astype(reflect_bank.dtype)
    chosen = jnp.einsum(
        "htb,hbd->htd", onehot, table, preferred_element_type=jnp.float32
    )
    vectors = chosen * lax.rsqrt(jnp.sum(chosen * chosen, axis=-1, keepdims=True) + 1e-06)
    blocks = vectors.reshape(heads, nblocks, BLK, HDIM)
    gram = jnp.einsum("hnkd,hnjd->hnkj", blocks, blocks, precision=HP)
    gram, q_local, k_local, v_local = lax.optimization_barrier((gram, q_local, k_local, v_local))
    coupling = 2.0 * jnp.triu(gram, 1)
    tri_factor = 2.0 * invert_unit_upper(coupling)
    spread = jnp.einsum("hnkj,hnje->hnke", tri_factor, blocks, precision=HP)
    eye_d = jnp.eye(HDIM, dtype=jnp.float32)
    block_mats = eye_d - jnp.einsum("hnkd,hnke->hnde", blocks, spread, precision=HP)
    lower_mask = jnp.tril(jnp.ones((BLK, BLK), dtype=jnp.bool_))

    inner_prefix, shard_prod = exclusive_blocks(block_mats)
    parts = 2 if heads % 2 == 0 else 1
    pw = width // parts
    w_other = [None] * parts
    if groups == 2:
        w_other = [
            lax.ppermute(out_weight[p * pw : (p + 1) * pw], "hg", SWAP) for p in range(parts)
        ]
    earlier_prod, v_all, w_other[0] = lax.optimization_barrier(
        (exclusive_shards(shard_prod, "ctx"), v_all, w_other[0])
    )

    def in_shard(matrix):
        split = matrix.astype(jnp.float32).reshape(nblocks, BLK, heads, HDIM).transpose(2, 0, 1, 3)
        proj = jnp.einsum("hnid,hnkd->hnik", split, blocks, precision=HP)
        proj = jnp.where(lower_mask, proj, 0.0)
        coef = jnp.einsum("hnik,hnrk->hnir", proj, tri_factor, precision=HP)
        inblock = split - jnp.einsum("hnir,hnrd->hnid", coef, blocks, precision=HP)
        moved = jnp.einsum("hnid,hned->hnie", inblock, inner_prefix, precision=HP)
        return moved.reshape(heads, rows, HDIM)

    kt_glob = jnp.einsum(
        "hie,hfe->hfi", in_shard(k_local), earlier_prod, precision=HP
    ).reshape(width, rows).astype(jnp.bfloat16)
    kt_parts = [
        lax.all_gather(kt_glob[p * pw : (p + 1) * pw], "ctx", axis=0, tiled=False)
        for p in range(parts)
    ]
    q_glob = (
        jnp.einsum("hie,hfe->hif", in_shard(q_local), earlier_prod, precision=HP)
        .transpose(1, 0, 2)
        .reshape(rows, width)
        .astype(jnp.bfloat16)
    )
    shard = lax.axis_index("ctx")
    attn = [
        flash_attend(q_glob[:, p * pw : (p + 1) * pw], kt_parts[p], v_all, p, shard, heads // parts)
        for p in range(parts)
    ]
    return project_out(attn, out_weight, w_other, groups)


def solution(mesh):
    placed = (
        P(("ctx", "hg"), None),
        P(("ctx", "hg"), None),
        P(("ctx", "hg"), None),
        P("ctx", "hg"),
        P(None, "hg"),
        P("hg", None),
    )
    return jax.shard_map(
        local, mesh=mesh, in_specs=placed, out_specs=P(("ctx", "hg"), None), check_vma=False
    )
```

```python
import math

import jax
import jax.numpy as jnp
from jax import lax
from jax.experimental import pallas as pl
from jax.experimental.pallas import tpu as pltpu
from jax.sharding import PartitionSpec as P

HDIM = 128
BLK = 32
GROUP = 1
HP = lax.Precision.HIGHEST


def mm(a, b):
    return jnp.einsum("...ij,...jk->...ik", a, b, precision=HP)


def invert_unit_upper(strict):
    eye_blk = jnp.eye(strict.shape[-1], dtype=jnp.float32)
    result = eye_blk - strict
    power = strict
    steps = strict.shape[-1].bit_length()
    for level in range(steps):
        power = mm(power, power)
        result = mm(result, eye_blk + power)
    return result


def exclusive_blocks(mats):
    heads, n, d, _ = mats.shape
    eye = jnp.broadcast_to(jnp.eye(d, dtype=jnp.float32), (heads, 1, d, d))
    acc = jnp.concatenate([eye, mats[:, :-1]], axis=1)
    shift = 1
    while shift < n:
        earlier = jnp.concatenate(
            [jnp.broadcast_to(eye, (heads, shift, d, d)), acc[:, : n - shift]], axis=1
        )
        acc = mm(earlier, acc)
        shift *= 2
    return acc, mm(acc[:, -1], mats[:, -1])


def exclusive_shards(mat, axis):
    length, here = lax.axis_size(axis), lax.axis_index(axis)
    eye = jnp.broadcast_to(jnp.eye(mat.shape[-1], dtype=jnp.float32), mat.shape)
    sizes = []
    rest = length
    for size in (2, 2):
        if rest % size == 0 and rest > size:
            sizes.append(size)
            rest //= size
    sizes.append(rest)
    block, before, stride = mat, eye, 1
    for level, size in enumerate(sizes):
        if size == 1:
            continue
        pos = (here // stride) % size
        last = level == len(sizes) - 1
        got = {}
        for dist in range(1, size):
            forward = [
                (i, i + dist * stride) for i in range(length) if (i // stride) % size + dist < size
            ]
            got[dist] = lax.ppermute(block, axis, forward)
            if not last:
                got[-dist] = lax.ppermute(
                    block, axis, [(b, a) for a, b in forward]
                )
        lead = eye
        for dist in range(size - 1, 0, -1):
            lead = mm(lead, jnp.where(pos >= dist, got[dist], eye))
        before = mm(lead, before)
        if not last:
            tail = block
            for dist in range(1, size):
                tail = mm(tail, jnp.where(pos + dist < size, got[-dist], eye))
            block = mm(lead, tail)
        stride *= size
    return before


def flash_attend(q_glob, kt_all, v_all, part, shard, heads, group=GROUP):
    rows, width = q_glob.shape
    nk = kt_all.shape[0]
    while nk % group:
        group //= 2
    nb = nk // group
    scale = 1.0 / math.sqrt(HDIM)

    def kernel(c_ref, q_ref, k_ref, v_ref, o_ref, m_sc, l_sc, acc_sc):
        j = pl.program_id(0)
        c = c_ref[0]

        @pl.when(j == 0)
        def _():
            m_sc[...] = jnp.full(m_sc.shape, -1e30, jnp.float32)
            l_sc[...] = jnp.zeros(l_sc.shape, jnp.float32)
            acc_sc[...] = jnp.zeros(acc_sc.shape, jnp.float32)

        def step(g, masked):
            for hh in range(heads):
                sl = slice(hh * HDIM, (hh + 1) * HDIM)
                qh = q_ref[:, sl]
                kh = k_ref[g, sl, :]
                vh = v_ref[g, :, sl]
                s = jnp.dot(qh, kh, preferred_element_type=jnp.float32) * scale
                if masked:
                    row = lax.broadcasted_iota(jnp.int32, s.shape, 0)
                    col = lax.broadcasted_iota(jnp.int32, s.shape, 1)
                    allowed = col <= row
                    s = jnp.where(allowed, s, -1e30)
                m_prev = m_sc[hh]
                m_new = jnp.maximum(m_prev, jnp.max(s, axis=1, keepdims=True))
                if s.shape[1] % HDIM == 0:
                    wide = jnp.concatenate([m_new] * (s.shape[1] // HDIM), axis=1)
                else:
                    wide = m_new[:, :1]
                p = jnp.exp(s - wide)
                if masked:
                    p = jnp.where(allowed, p, 0.0)
                fade = jnp.exp(m_prev - m_new)
                l_sc[hh] = l_sc[hh] * fade + jnp.sum(p, axis=1, keepdims=True)
                acc_sc[hh] = acc_sc[hh] * fade + jnp.dot(
                    p.astype(jnp.bfloat16), vh, preferred_element_type=jnp.float32
                )
                m_sc[hh] = m_new

        for g in range(group):
            here = j * group + g

            @pl.when(here < c)
            def _():
                step(g, False)

            @pl.when(here == c)
            def _():
                step(g, True)

        @pl.when(j == nb - 1)
        def _():
            for hh in range(heads):
                sl = slice(hh * HDIM, (hh + 1) * HDIM)
                o_ref[:, sl] = (acc_sc[hh] / l_sc[hh]).astype(o_ref.dtype)

    grid_spec = pltpu.PrefetchScalarGridSpec(
        num_scalar_prefetch=1,
        grid=(nb,),
        in_specs=[
            pl.BlockSpec((rows, width), lambda j, c: (0, 0)),
            pl.BlockSpec((group, width, rows), lambda j, c: (jnp.minimum(j, c[0] // group), 0, 0)),
            pl.BlockSpec((group, rows, width), lambda j, c: (jnp.minimum(j, c[0] // group), 0, part)),
        ],
        out_specs=pl.BlockSpec((rows, width), lambda j, c: (0, 0)),
        scratch_shapes=[
            pltpu.VMEM((heads, rows, HDIM), jnp.float32),
            pltpu.VMEM((heads, rows, HDIM), jnp.float32),
            pltpu.VMEM((heads, rows, HDIM), jnp.float32),
        ],
    )
    return pl.pallas_call(
        kernel,
        grid_spec=grid_spec,
        out_shape=jax.ShapeDtypeStruct((rows, width), jnp.bfloat16),
        compiler_params=pltpu.CompilerParams(dimension_semantics=("arbitrary",)),
    )(jnp.reshape(shard, (1,)).astype(jnp.int32), q_glob, kt_all, v_all)


SWAP = [(0, 1), (1, 0)]


def exchange_heads(x, groups, width):
    if groups != 2:
        split = x.reshape(x.shape[0], groups, width)
        return lax.all_to_all(split, "hg", split_axis=1, concat_axis=0, tiled=True)[:, 0]
    first = lax.axis_index("hg") == 0
    own = jnp.where(first, x[:, :width], x[:, width:])
    got = lax.ppermute(jnp.where(first, x[:, width:], x[:, :width]), "hg", SWAP)
    return jnp.where(
        first, jnp.concatenate([own, got], axis=0), jnp.concatenate([got, own], axis=0)
    )


def project_out(parts, out_weight, w_other, groups):
    if groups != 2:
        return lax.psum_scatter(
            jnp.dot(
                jnp.concatenate(parts, axis=1), out_weight, preferred_element_type=jnp.float32
            ).astype(jnp.bfloat16),
            "hg",
            scatter_dimension=0,
            tiled=True,
        )
    half = parts[0].shape[0] // 2
    first = lax.axis_index("hg") == 0
    got = [
        lax.ppermute(jnp.where(first, a[half:], a[:half]), "hg", SWAP) for a in parts
    ]
    mine = jnp.concatenate([jnp.where(first, a[:half], a[half:]) for a in parts], axis=1)
    total = jnp.dot(mine, out_weight, preferred_element_type=jnp.float32)
    for a, w in zip(got, w_other):
        total = total + jnp.dot(a, w, preferred_element_type=jnp.float32)
    return total.astype(jnp.bfloat16)


def local(queries, keys, values, reflect_ids, reflect_bank, out_weight):
    groups = lax.axis_size("hg")
    heads = reflect_ids.shape[1]
    width = heads * HDIM
    q_local, k_local, v_local = (exchange_heads(x, groups, width) for x in (queries, keys, values))
    rows = q_local.shape[0]
    v_all = lax.all_gather(v_local, "ctx", axis=0, tiled=False)

    nblocks = rows // BLK
    bank = reflect_bank.shape[0]
    table = reflect_bank.reshape(bank, heads, HDIM).transpose(1, 0, 2)
    onehot = (
        reflect_ids.T[:, :, None] == lax.broadcasted_iota(jnp.int32, (1, 1, bank), 2)
    ).astype(reflect_bank.dtype)
    chosen = jnp.einsum(
        "htb,hbd->htd", onehot, table, preferred_element_type=jnp.float32
    )
    vectors = chosen * lax.rsqrt(jnp.sum(chosen * chosen, axis=-1, keepdims=True) + 1e-06)
    blocks = vectors.reshape(heads, nblocks, BLK, HDIM)
    gram = jnp.einsum("hnkd,hnjd->hnkj", blocks, blocks, precision=HP)
    gram, q_local, k_local, v_local = lax.optimization_barrier((gram, q_local, k_local, v_local))
    coupling = 2.0 * jnp.triu(gram, 1)
    tri_factor = 2.0 * invert_unit_upper(coupling)
    spread = jnp.einsum("hnkj,hnje->hnke", tri_factor, blocks, precision=HP)
    eye_d = jnp.eye(HDIM, dtype=jnp.float32)
    block_mats = eye_d - jnp.einsum("hnkd,hnke->hnde", blocks, spread, precision=HP)
    lower_mask = jnp.tril(jnp.ones((BLK, BLK), dtype=jnp.bool_))

    inner_prefix, shard_prod = exclusive_blocks(block_mats)
    parts = 2 if heads % 2 == 0 else 1
    pw = width // parts
    w_other = [None] * parts
    if groups == 2:
        w_other = [
            lax.ppermute(out_weight[p * pw : (p + 1) * pw], "hg", SWAP) for p in range(parts)
        ]
    earlier_prod, v_all = lax.optimization_barrier((exclusive_shards(shard_prod, "ctx"), v_all))

    def in_shard(matrix):
        split = matrix.astype(jnp.float32).reshape(nblocks, BLK, heads, HDIM).transpose(2, 0, 1, 3)
        proj = jnp.einsum("hnid,hnkd->hnik", split, blocks, precision=HP)
        proj = jnp.where(lower_mask, proj, 0.0)
        coef = jnp.einsum("hnik,hnrk->hnir", proj, tri_factor, precision=HP)
        inblock = split - jnp.einsum("hnir,hnrd->hnid", coef, blocks, precision=HP)
        moved = jnp.einsum("hnid,hned->hnie", inblock, inner_prefix, precision=HP)
        return moved.reshape(heads, rows, HDIM)

    kt_glob = jnp.einsum(
        "hie,hfe->hfi", in_shard(k_local), earlier_prod, precision=HP
    ).reshape(width, rows).astype(jnp.bfloat16)
    kt_glob, w_other[0] = lax.optimization_barrier((kt_glob, w_other[0]))
    kt_parts = [
        lax.all_gather(kt_glob[p * pw : (p + 1) * pw], "ctx", axis=0, tiled=False)
        for p in range(parts)
    ]
    q_glob = (
        jnp.einsum("hie,hfe->hif", in_shard(q_local), earlier_prod, precision=HP)
        .transpose(1, 0, 2)
        .reshape(rows, width)
        .astype(jnp.bfloat16)
    )
    shard = lax.axis_index("ctx")
    attn = [
        flash_attend(q_glob[:, p * pw : (p + 1) * pw], kt_parts[p], v_all, p, shard, heads // parts)
        for p in range(parts)
    ]
    return project_out(attn, out_weight, w_other, groups)


def solution(mesh):
    placed = (
        P(("ctx", "hg"), None),
        P(("ctx", "hg"), None),
        P(("ctx", "hg"), None),
        P("ctx", "hg"),
        P(None, "hg"),
        P("hg", None),
    )
    return jax.shard_map(
        local, mesh=mesh, in_specs=placed, out_specs=P(("ctx", "hg"), None), check_vma=False
    )
```

```python
import math

import jax
import jax.numpy as jnp
from jax import lax
from jax.experimental import pallas as pl
from jax.experimental.pallas import tpu as pltpu
from jax.sharding import PartitionSpec as P

HDIM = 128
BLK = 32
GROUP = 1
HP = lax.Precision.HIGHEST


def mm(a, b):
    return jnp.einsum("...ij,...jk->...ik", a, b, precision=HP)


def invert_unit_upper(strict):
    eye_blk = jnp.eye(strict.shape[-1], dtype=jnp.float32)
    result = eye_blk - strict
    power = strict
    steps = strict.shape[-1].bit_length()
    for level in range(steps):
        power = mm(power, power)
        result = mm(result, eye_blk + power)
    return result


def exclusive_blocks(mats):
    heads, n, d, _ = mats.shape
    eye = jnp.broadcast_to(jnp.eye(d, dtype=jnp.float32), (heads, 1, d, d))
    acc = jnp.concatenate([eye, mats[:, :-1]], axis=1)
    shift = 1
    while shift < n:
        earlier = jnp.concatenate(
            [jnp.broadcast_to(eye, (heads, shift, d, d)), acc[:, : n - shift]], axis=1
        )
        acc = mm(earlier, acc)
        shift *= 2
    return acc, mm(acc[:, -1], mats[:, -1])


def exclusive_shards(mat, axis):
    length, here = lax.axis_size(axis), lax.axis_index(axis)
    eye = jnp.broadcast_to(jnp.eye(mat.shape[-1], dtype=jnp.float32), mat.shape)
    sizes = []
    rest = length
    for size in (2, 2):
        if rest % size == 0 and rest > size:
            sizes.append(size)
            rest //= size
    sizes.append(rest)
    block, before, stride = mat, eye, 1
    for level, size in enumerate(sizes):
        if size == 1:
            continue
        pos = (here // stride) % size
        last = level == len(sizes) - 1
        got = {}
        for dist in range(1, size):
            forward = [
                (i, i + dist * stride) for i in range(length) if (i // stride) % size + dist < size
            ]
            got[dist] = lax.ppermute(block, axis, forward)
            if not last:
                got[-dist] = lax.ppermute(
                    block, axis, [(b, a) for a, b in forward]
                )
        lead = eye
        for dist in range(size - 1, 0, -1):
            lead = mm(lead, jnp.where(pos >= dist, got[dist], eye))
        before = mm(lead, before)
        if not last:
            tail = block
            for dist in range(1, size):
                tail = mm(tail, jnp.where(pos + dist < size, got[-dist], eye))
            block = mm(lead, tail)
        stride *= size
    return before


def flash_attend(q_glob, kt_all, v_all, part, shard, heads, group=GROUP):
    rows, width = q_glob.shape
    nk = kt_all.shape[0]
    while nk % group:
        group //= 2
    nb = nk // group
    scale = 1.0 / math.sqrt(HDIM)

    def kernel(c_ref, q_ref, k_ref, v_ref, o_ref, m_sc, l_sc, acc_sc):
        j = pl.program_id(0)
        c = c_ref[0]

        @pl.when(j == 0)
        def _():
            m_sc[...] = jnp.full(m_sc.shape, -1e30, jnp.float32)
            l_sc[...] = jnp.zeros(l_sc.shape, jnp.float32)
            acc_sc[...] = jnp.zeros(acc_sc.shape, jnp.float32)

        def step(g, masked):
            for hh in range(heads):
                sl = slice(hh * HDIM, (hh + 1) * HDIM)
                qh = q_ref[:, sl]
                kh = k_ref[g, sl, :]
                vh = v_ref[g, :, sl]
                s = jnp.dot(qh, kh, preferred_element_type=jnp.float32) * scale
                if masked:
                    row = lax.broadcasted_iota(jnp.int32, s.shape, 0)
                    col = lax.broadcasted_iota(jnp.int32, s.shape, 1)
                    allowed = col <= row
                    s = jnp.where(allowed, s, -1e30)
                m_prev = m_sc[hh]
                m_new = jnp.maximum(m_prev, jnp.max(s, axis=1, keepdims=True))
                if s.shape[1] % HDIM == 0:
                    wide = jnp.concatenate([m_new] * (s.shape[1] // HDIM), axis=1)
                else:
                    wide = m_new[:, :1]
                p = jnp.exp(s - wide)
                if masked:
                    p = jnp.where(allowed, p, 0.0)
                fade = jnp.exp(m_prev - m_new)
                l_sc[hh] = l_sc[hh] * fade + jnp.sum(p, axis=1, keepdims=True)
                acc_sc[hh] = acc_sc[hh] * fade + jnp.dot(
                    p.astype(jnp.bfloat16), vh, preferred_element_type=jnp.float32
                )
                m_sc[hh] = m_new

        for g in range(group):
            here = j * group + g

            @pl.when(here < c)
            def _():
                step(g, False)

            @pl.when(here == c)
            def _():
                step(g, True)

        @pl.when(j == nb - 1)
        def _():
            for hh in range(heads):
                sl = slice(hh * HDIM, (hh + 1) * HDIM)
                o_ref[:, sl] = (acc_sc[hh] / l_sc[hh]).astype(o_ref.dtype)

    grid_spec = pltpu.PrefetchScalarGridSpec(
        num_scalar_prefetch=1,
        grid=(nb,),
        in_specs=[
            pl.BlockSpec((rows, width), lambda j, c: (0, 0)),
            pl.BlockSpec((group, width, rows), lambda j, c: (jnp.minimum(j, c[0] // group), 0, 0)),
            pl.BlockSpec((group, rows, width), lambda j, c: (jnp.minimum(j, c[0] // group), 0, part)),
        ],
        out_specs=pl.BlockSpec((rows, width), lambda j, c: (0, 0)),
        scratch_shapes=[
            pltpu.VMEM((heads, rows, HDIM), jnp.float32),
            pltpu.VMEM((heads, rows, HDIM), jnp.float32),
            pltpu.VMEM((heads, rows, HDIM), jnp.float32),
        ],
    )
    return pl.pallas_call(
        kernel,
        grid_spec=grid_spec,
        out_shape=jax.ShapeDtypeStruct((rows, width), jnp.bfloat16),
        compiler_params=pltpu.CompilerParams(dimension_semantics=("arbitrary",)),
    )(jnp.reshape(shard, (1,)).astype(jnp.int32), q_glob, kt_all, v_all)


SWAP = [(0, 1), (1, 0)]


def exchange_heads(x, groups, width):
    if groups != 2:
        split = x.reshape(x.shape[0], groups, width)
        return lax.all_to_all(split, "hg", split_axis=1, concat_axis=0, tiled=True)[:, 0]
    first = lax.axis_index("hg") == 0
    own = jnp.where(first, x[:, :width], x[:, width:])
    got = lax.ppermute(jnp.where(first, x[:, width:], x[:, :width]), "hg", SWAP)
    return jnp.where(
        first, jnp.concatenate([own, got], axis=0), jnp.concatenate([got, own], axis=0)
    )


def project_out(parts, out_weight, w_other, groups):
    if groups != 2:
        return lax.psum_scatter(
            jnp.dot(
                jnp.concatenate(parts, axis=1), out_weight, preferred_element_type=jnp.float32
            ).astype(jnp.bfloat16),
            "hg",
            scatter_dimension=0,
            tiled=True,
        )
    half = parts[0].shape[0] // 2
    first = lax.axis_index("hg") == 0
    got = [
        lax.ppermute(jnp.where(first, a[half:], a[:half]), "hg", SWAP) for a in parts
    ]
    mine = jnp.concatenate([jnp.where(first, a[:half], a[half:]) for a in parts], axis=1)
    total = jnp.dot(mine, out_weight, preferred_element_type=jnp.float32)
    got = jnp.concatenate(got, axis=1)
    cut = w_other[0].shape[0]
    total = total + jnp.dot(got[:, :cut], w_other[0], preferred_element_type=jnp.float32)
    if w_other[1] is not None:
        total = total + jnp.dot(got[:, cut:], w_other[1], preferred_element_type=jnp.float32)
    return total.astype(jnp.bfloat16)


def local(queries, keys, values, reflect_ids, reflect_bank, out_weight):
    groups = lax.axis_size("hg")
    heads = reflect_ids.shape[1]
    width = heads * HDIM
    q_local, k_local, v_local = (exchange_heads(x, groups, width) for x in (queries, keys, values))
    rows = q_local.shape[0]
    v_all = lax.all_gather(v_local, "ctx", axis=0, tiled=False)

    nblocks = rows // BLK
    bank = reflect_bank.shape[0]
    table = reflect_bank.reshape(bank, heads, HDIM).transpose(1, 0, 2)
    onehot = (
        reflect_ids.T[:, :, None] == lax.broadcasted_iota(jnp.int32, (1, 1, bank), 2)
    ).astype(reflect_bank.dtype)
    chosen = jnp.einsum(
        "htb,hbd->htd", onehot, table, preferred_element_type=jnp.float32
    )
    vectors = chosen * lax.rsqrt(jnp.sum(chosen * chosen, axis=-1, keepdims=True) + 1e-06)
    blocks = vectors.reshape(heads, nblocks, BLK, HDIM)
    gram = jnp.einsum("hnkd,hnjd->hnkj", blocks, blocks, precision=HP)
    gram, q_local, k_local, v_local = lax.optimization_barrier((gram, q_local, k_local, v_local))
    coupling = 2.0 * jnp.triu(gram, 1)
    tri_factor = 2.0 * invert_unit_upper(coupling)
    spread = jnp.einsum("hnkj,hnje->hnke", tri_factor, blocks, precision=HP)
    eye_d = jnp.eye(HDIM, dtype=jnp.float32)
    block_mats = eye_d - jnp.einsum("hnkd,hnke->hnde", blocks, spread, precision=HP)
    lower_mask = jnp.tril(jnp.ones((BLK, BLK), dtype=jnp.bool_))

    inner_prefix, shard_prod = exclusive_blocks(block_mats)
    parts = 2 if heads % 2 == 0 else 1
    pw = width // parts
    cut = max(1, (3 * heads) // 8) * HDIM
    w_other = [None, None]
    if groups == 2:
        w_other = [lax.ppermute(out_weight[:cut], "hg", SWAP), None]
        if cut < width:
            w_other[1] = lax.ppermute(out_weight[cut:], "hg", SWAP)
    earlier_prod, v_all, w_other[0] = lax.optimization_barrier(
        (exclusive_shards(shard_prod, "ctx"), v_all, w_other[0])
    )

    def in_shard(matrix):
        split = matrix.astype(jnp.float32).reshape(nblocks, BLK, heads, HDIM).transpose(2, 0, 1, 3)
        proj = jnp.einsum("hnid,hnkd->hnik", split, blocks, precision=HP)
        proj = jnp.where(lower_mask, proj, 0.0)
        coef = jnp.einsum("hnik,hnrk->hnir", proj, tri_factor, precision=HP)
        inblock = split - jnp.einsum("hnir,hnrd->hnid", coef, blocks, precision=HP)
        moved = jnp.einsum("hnid,hned->hnie", inblock, inner_prefix, precision=HP)
        return moved.reshape(heads, rows, HDIM)

    kt_glob = jnp.einsum(
        "hie,hfe->hfi", in_shard(k_local), earlier_prod, precision=HP
    ).reshape(width, rows).astype(jnp.bfloat16)
    kt_parts = [
        lax.all_gather(kt_glob[p * pw : (p + 1) * pw], "ctx", axis=0, tiled=False)
        for p in range(parts)
    ]
    q_glob = (
        jnp.einsum("hie,hfe->hif", in_shard(q_local), earlier_prod, precision=HP)
        .transpose(1, 0, 2)
        .reshape(rows, width)
        .astype(jnp.bfloat16)
    )
    shard = lax.axis_index("ctx")
    attn = [
        flash_attend(q_glob[:, p * pw : (p + 1) * pw], kt_parts[p], v_all, p, shard, heads // parts)
        for p in range(parts)
    ]
    return project_out(attn, out_weight, w_other, groups)


def solution(mesh):
    placed = (
        P(("ctx", "hg"), None),
        P(("ctx", "hg"), None),
        P(("ctx", "hg"), None),
        P("ctx", "hg"),
        P(None, "hg"),
        P("hg", None),
    )
    return jax.shard_map(
        local, mesh=mesh, in_specs=placed, out_specs=P(("ctx", "hg"), None), check_vma=False
    )
```

```python
import math

import jax
import jax.numpy as jnp
from jax import lax
from jax.experimental import pallas as pl
from jax.experimental.pallas import tpu as pltpu
from jax.sharding import PartitionSpec as P

HDIM = 128
BLK = 32
GROUP = 1
HP = lax.Precision.HIGHEST


def mm(a, b):
    return jnp.einsum("...ij,...jk->...ik", a, b, precision=HP)


def invert_unit_upper(strict):
    eye_blk = jnp.eye(strict.shape[-1], dtype=jnp.float32)
    result = eye_blk - strict
    power = strict
    steps = strict.shape[-1].bit_length()
    for level in range(steps):
        power = mm(power, power)
        result = mm(result, eye_blk + power)
    return result


def exclusive_blocks(mats):
    heads, n, d, _ = mats.shape
    eye = jnp.broadcast_to(jnp.eye(d, dtype=jnp.float32), (heads, 1, d, d))
    acc = jnp.concatenate([eye, mats[:, :-1]], axis=1)
    shift = 1
    while shift < n:
        earlier = jnp.concatenate(
            [jnp.broadcast_to(eye, (heads, shift, d, d)), acc[:, : n - shift]], axis=1
        )
        acc = mm(earlier, acc)
        shift *= 2
    return acc, mm(acc[:, -1], mats[:, -1])


def exclusive_shards(mat, axis):
    length, here = lax.axis_size(axis), lax.axis_index(axis)
    eye = jnp.broadcast_to(jnp.eye(mat.shape[-1], dtype=jnp.float32), mat.shape)
    sizes = []
    rest = length
    for size in (2, 2):
        if rest % size == 0 and rest > size:
            sizes.append(size)
            rest //= size
    sizes.append(rest)
    block, before, stride = mat, eye, 1
    for level, size in enumerate(sizes):
        if size == 1:
            continue
        pos = (here // stride) % size
        last = level == len(sizes) - 1
        got = {}
        for dist in range(1, size):
            forward = [
                (i, i + dist * stride) for i in range(length) if (i // stride) % size + dist < size
            ]
            got[dist] = lax.ppermute(block, axis, forward)
            if not last:
                got[-dist] = lax.ppermute(
                    block, axis, [(b, a) for a, b in forward]
                )
        lead = eye
        for dist in range(size - 1, 0, -1):
            lead = mm(lead, jnp.where(pos >= dist, got[dist], eye))
        before = mm(lead, before)
        if not last:
            tail = block
            for dist in range(1, size):
                tail = mm(tail, jnp.where(pos + dist < size, got[-dist], eye))
            block = mm(lead, tail)
        stride *= size
    return before


def flash_attend(q_glob, kt_all, v_all, part, shard, heads, group=GROUP):
    rows, width = q_glob.shape
    nk = kt_all.shape[0]
    while nk % group:
        group //= 2
    nb = nk // group
    scale = 1.0 / math.sqrt(HDIM)

    def kernel(c_ref, q_ref, k_ref, v_ref, o_ref, m_sc, l_sc, acc_sc):
        j = pl.program_id(0)
        c = c_ref[0]

        @pl.when(j == 0)
        def _():
            m_sc[...] = jnp.full(m_sc.shape, -1e30, jnp.float32)
            l_sc[...] = jnp.zeros(l_sc.shape, jnp.float32)
            acc_sc[...] = jnp.zeros(acc_sc.shape, jnp.float32)

        def step(g, masked):
            for hh in range(heads):
                sl = slice(hh * HDIM, (hh + 1) * HDIM)
                qh = q_ref[:, sl]
                kh = k_ref[g, sl, :]
                vh = v_ref[g, :, sl]
                s = jnp.dot(qh, kh, preferred_element_type=jnp.float32) * scale
                if masked:
                    row = lax.broadcasted_iota(jnp.int32, s.shape, 0)
                    col = lax.broadcasted_iota(jnp.int32, s.shape, 1)
                    allowed = col <= row
                    s = jnp.where(allowed, s, -1e30)
                m_prev = m_sc[hh]
                m_new = jnp.maximum(m_prev, jnp.max(s, axis=1, keepdims=True))
                if s.shape[1] % HDIM == 0:
                    wide = jnp.concatenate([m_new] * (s.shape[1] // HDIM), axis=1)
                else:
                    wide = m_new[:, :1]
                p = jnp.exp(s - wide)
                if masked:
                    p = jnp.where(allowed, p, 0.0)
                fade = jnp.exp(m_prev - m_new)
                l_sc[hh] = l_sc[hh] * fade + jnp.sum(p, axis=1, keepdims=True)
                acc_sc[hh] = acc_sc[hh] * fade + jnp.dot(
                    p.astype(jnp.bfloat16), vh, preferred_element_type=jnp.float32
                )
                m_sc[hh] = m_new

        for g in range(group):
            here = j * group + g

            @pl.when(here < c)
            def _():
                step(g, False)

            @pl.when(here == c)
            def _():
                step(g, True)

        @pl.when(j == nb - 1)
        def _():
            for hh in range(heads):
                sl = slice(hh * HDIM, (hh + 1) * HDIM)
                o_ref[:, sl] = (acc_sc[hh] / l_sc[hh]).astype(o_ref.dtype)

    grid_spec = pltpu.PrefetchScalarGridSpec(
        num_scalar_prefetch=1,
        grid=(nb,),
        in_specs=[
            pl.BlockSpec((rows, width), lambda j, c: (0, 0)),
            pl.BlockSpec((group, width, rows), lambda j, c: (jnp.minimum(j, c[0] // group), 0, 0)),
            pl.BlockSpec((group, rows, width), lambda j, c: (jnp.minimum(j, c[0] // group), 0, part)),
        ],
        out_specs=pl.BlockSpec((rows, width), lambda j, c: (0, 0)),
        scratch_shapes=[
            pltpu.VMEM((heads, rows, HDIM), jnp.float32),
            pltpu.VMEM((heads, rows, HDIM), jnp.float32),
            pltpu.VMEM((heads, rows, HDIM), jnp.float32),
        ],
    )
    return pl.pallas_call(
        kernel,
        grid_spec=grid_spec,
        out_shape=jax.ShapeDtypeStruct((rows, width), jnp.bfloat16),
        compiler_params=pltpu.CompilerParams(dimension_semantics=("arbitrary",)),
    )(jnp.reshape(shard, (1,)).astype(jnp.int32), q_glob, kt_all, v_all)


SWAP = [(0, 1), (1, 0)]


def exchange_heads(x, groups, width):
    if groups != 2:
        split = x.reshape(x.shape[0], groups, width)
        return lax.all_to_all(split, "hg", split_axis=1, concat_axis=0, tiled=True)[:, 0]
    first = lax.axis_index("hg") == 0
    own = jnp.where(first, x[:, :width], x[:, width:])
    got = lax.ppermute(jnp.where(first, x[:, width:], x[:, :width]), "hg", SWAP)
    return jnp.where(
        first, jnp.concatenate([own, got], axis=0), jnp.concatenate([got, own], axis=0)
    )


def project_out(parts, out_weight, w_other, groups):
    if groups != 2:
        return lax.psum_scatter(
            jnp.dot(
                jnp.concatenate(parts, axis=1), out_weight, preferred_element_type=jnp.float32
            ).astype(jnp.bfloat16),
            "hg",
            scatter_dimension=0,
            tiled=True,
        )
    half = parts[0].shape[0] // 2
    first = lax.axis_index("hg") == 0
    got = [
        lax.ppermute(jnp.where(first, a[half:], a[:half]), "hg", SWAP) for a in parts
    ]
    mine = jnp.concatenate([jnp.where(first, a[:half], a[half:]) for a in parts], axis=1)
    total = jnp.dot(mine, out_weight, preferred_element_type=jnp.float32)
    got = jnp.concatenate(got, axis=1)
    cut = w_other[0].shape[0]
    total = total + jnp.dot(got[:, :cut], w_other[0], preferred_element_type=jnp.float32)
    if w_other[1] is not None:
        total = total + jnp.dot(got[:, cut:], w_other[1], preferred_element_type=jnp.float32)
    return total.astype(jnp.bfloat16)


def local(queries, keys, values, reflect_ids, reflect_bank, out_weight):
    groups = lax.axis_size("hg")
    heads = reflect_ids.shape[1]
    width = heads * HDIM
    q_local, k_local, v_local = (exchange_heads(x, groups, width) for x in (queries, keys, values))
    rows = q_local.shape[0]
    v_all = lax.all_gather(v_local, "ctx", axis=0, tiled=False)

    nblocks = rows // BLK
    bank = reflect_bank.shape[0]
    table = reflect_bank.reshape(bank, heads, HDIM).transpose(1, 0, 2)
    onehot = (
        reflect_ids.T[:, :, None] == lax.broadcasted_iota(jnp.int32, (1, 1, bank), 2)
    ).astype(reflect_bank.dtype)
    chosen = jnp.einsum(
        "htb,hbd->htd", onehot, table, preferred_element_type=jnp.float32
    )
    vectors = chosen * lax.rsqrt(jnp.sum(chosen * chosen, axis=-1, keepdims=True) + 1e-06)
    blocks = vectors.reshape(heads, nblocks, BLK, HDIM)
    gram = jnp.einsum("hnkd,hnjd->hnkj", blocks, blocks, precision=HP)
    cut = max(1, (3 * heads) // 8) * HDIM
    w_rest = out_weight[cut:] if groups == 2 and cut < width else None
    gram, q_local, k_local, v_local, w_rest = lax.optimization_barrier(
        (gram, q_local, k_local, v_local, w_rest)
    )
    coupling = 2.0 * jnp.triu(gram, 1)
    tri_factor = 2.0 * invert_unit_upper(coupling)
    spread = jnp.einsum("hnkj,hnje->hnke", tri_factor, blocks, precision=HP)
    eye_d = jnp.eye(HDIM, dtype=jnp.float32)
    block_mats = eye_d - jnp.einsum("hnkd,hnke->hnde", blocks, spread, precision=HP)
    lower_mask = jnp.tril(jnp.ones((BLK, BLK), dtype=jnp.bool_))

    inner_prefix, shard_prod = exclusive_blocks(block_mats)
    parts = 2 if heads % 2 == 0 else 1
    pw = width // parts
    w_other = [None, None]
    if groups == 2:
        w_other = [lax.ppermute(out_weight[:cut], "hg", SWAP), None]
        if w_rest is not None:
            w_other[1] = lax.ppermute(w_rest, "hg", SWAP)
    earlier_prod, v_all, w_other[0] = lax.optimization_barrier(
        (exclusive_shards(shard_prod, "ctx"), v_all, w_other[0])
    )

    def in_shard(matrix):
        split = matrix.astype(jnp.float32).reshape(nblocks, BLK, heads, HDIM).transpose(2, 0, 1, 3)
        proj = jnp.einsum("hnid,hnkd->hnik", split, blocks, precision=HP)
        proj = jnp.where(lower_mask, proj, 0.0)
        coef = jnp.einsum("hnik,hnrk->hnir", proj, tri_factor, precision=HP)
        inblock = split - jnp.einsum("hnir,hnrd->hnid", coef, blocks, precision=HP)
        moved = jnp.einsum("hnid,hned->hnie", inblock, inner_prefix, precision=HP)
        return moved.reshape(heads, rows, HDIM)

    kt_glob = jnp.einsum(
        "hie,hfe->hfi", in_shard(k_local), earlier_prod, precision=HP
    ).reshape(width, rows).astype(jnp.bfloat16)
    kt_parts = [
        lax.all_gather(kt_glob[p * pw : (p + 1) * pw], "ctx", axis=0, tiled=False)
        for p in range(parts)
    ]
    q_glob = (
        jnp.einsum("hie,hfe->hif", in_shard(q_local), earlier_prod, precision=HP)
        .transpose(1, 0, 2)
        .reshape(rows, width)
        .astype(jnp.bfloat16)
    )
    shard = lax.axis_index("ctx")
    attn = [
        flash_attend(q_glob[:, p * pw : (p + 1) * pw], kt_parts[p], v_all, p, shard, heads // parts)
        for p in range(parts)
    ]
    return project_out(attn, out_weight, w_other, groups)


def solution(mesh):
    placed = (
        P(("ctx", "hg"), None),
        P(("ctx", "hg"), None),
        P(("ctx", "hg"), None),
        P("ctx", "hg"),
        P(None, "hg"),
        P("hg", None),
    )
    return jax.shard_map(
        local, mesh=mesh, in_specs=placed, out_specs=P(("ctx", "hg"), None), check_vma=False
    )
```

```python
import math

import jax
import jax.numpy as jnp
from jax import lax
from jax.experimental import pallas as pl
from jax.experimental.pallas import tpu as pltpu
from jax.sharding import PartitionSpec as P

HDIM = 128
BLK = 32
GROUP = 1
HP = lax.Precision.HIGHEST


def mm(a, b):
    return jnp.einsum("...ij,...jk->...ik", a, b, precision=HP)


def invert_unit_upper(strict):
    eye_blk = jnp.eye(strict.shape[-1], dtype=jnp.float32)
    result = eye_blk - strict
    power = strict
    steps = strict.shape[-1].bit_length()
    for level in range(steps):
        power = mm(power, power)
        result = mm(result, eye_blk + power)
    return result


def exclusive_blocks(mats):
    heads, n, d, _ = mats.shape
    eye = jnp.broadcast_to(jnp.eye(d, dtype=jnp.float32), (heads, 1, d, d))
    acc = jnp.concatenate([eye, mats[:, :-1]], axis=1)
    shift = 1
    while shift < n:
        earlier = jnp.concatenate(
            [jnp.broadcast_to(eye, (heads, shift, d, d)), acc[:, : n - shift]], axis=1
        )
        acc = mm(earlier, acc)
        shift *= 2
    return acc, mm(acc[:, -1], mats[:, -1])


def exclusive_shards(mat, axis):
    length, here = lax.axis_size(axis), lax.axis_index(axis)
    eye = jnp.broadcast_to(jnp.eye(mat.shape[-1], dtype=jnp.float32), mat.shape)
    sizes = []
    rest = length
    for size in (2, 2):
        if rest % size == 0 and rest > size:
            sizes.append(size)
            rest //= size
    sizes.append(rest)
    block, before, stride = mat, eye, 1
    for level, size in enumerate(sizes):
        if size == 1:
            continue
        pos = (here // stride) % size
        last = level == len(sizes) - 1
        got = {}
        for dist in range(1, size):
            forward = [
                (i, i + dist * stride) for i in range(length) if (i // stride) % size + dist < size
            ]
            got[dist] = lax.ppermute(block, axis, forward)
            if not last:
                got[-dist] = lax.ppermute(
                    block, axis, [(b, a) for a, b in forward]
                )
        lead = eye
        for dist in range(size - 1, 0, -1):
            lead = mm(lead, jnp.where(pos >= dist, got[dist], eye))
        before = mm(lead, before)
        if not last:
            tail = block
            for dist in range(1, size):
                tail = mm(tail, jnp.where(pos + dist < size, got[-dist], eye))
            block = mm(lead, tail)
        stride *= size
    return before


def flash_attend(q_glob, kt_all, v_all, part, shard, heads, group=GROUP):
    rows, width = q_glob.shape
    nk = kt_all.shape[0]
    while nk % group:
        group //= 2
    nb = nk // group
    scale = 1.0 / math.sqrt(HDIM)

    def kernel(c_ref, q_ref, k_ref, v_ref, o_ref, m_sc, l_sc, acc_sc):
        j = pl.program_id(0)
        c = c_ref[0]

        @pl.when(j == 0)
        def _():
            m_sc[...] = jnp.full(m_sc.shape, -1e30, jnp.float32)
            l_sc[...] = jnp.zeros(l_sc.shape, jnp.float32)
            acc_sc[...] = jnp.zeros(acc_sc.shape, jnp.float32)

        def step(g, masked):
            for hh in range(heads):
                sl = slice(hh * HDIM, (hh + 1) * HDIM)
                qh = q_ref[:, sl]
                kh = k_ref[g, sl, :]
                vh = v_ref[g, :, sl]
                s = jnp.dot(qh, kh, preferred_element_type=jnp.float32) * scale
                if masked:
                    row = lax.broadcasted_iota(jnp.int32, s.shape, 0)
                    col = lax.broadcasted_iota(jnp.int32, s.shape, 1)
                    allowed = col <= row
                    s = jnp.where(allowed, s, -1e30)
                m_prev = m_sc[hh]
                m_new = jnp.maximum(m_prev, jnp.max(s, axis=1, keepdims=True))
                if s.shape[1] % HDIM == 0:
                    wide = jnp.concatenate([m_new] * (s.shape[1] // HDIM), axis=1)
                else:
                    wide = m_new[:, :1]
                p = jnp.exp(s - wide)
                if masked:
                    p = jnp.where(allowed, p, 0.0)
                fade = jnp.exp(m_prev - m_new)
                l_sc[hh] = l_sc[hh] * fade + jnp.sum(p, axis=1, keepdims=True)
                acc_sc[hh] = acc_sc[hh] * fade + jnp.dot(
                    p.astype(jnp.bfloat16), vh, preferred_element_type=jnp.float32
                )
                m_sc[hh] = m_new

        for g in range(group):
            here = j * group + g

            @pl.when(here < c)
            def _():
                step(g, False)

            @pl.when(here == c)
            def _():
                step(g, True)

        @pl.when(j == nb - 1)
        def _():
            for hh in range(heads):
                sl = slice(hh * HDIM, (hh + 1) * HDIM)
                o_ref[:, sl] = (acc_sc[hh] / l_sc[hh]).astype(o_ref.dtype)

    grid_spec = pltpu.PrefetchScalarGridSpec(
        num_scalar_prefetch=1,
        grid=(nb,),
        in_specs=[
            pl.BlockSpec((rows, width), lambda j, c: (0, 0)),
            pl.BlockSpec((group, width, rows), lambda j, c: (jnp.minimum(j, c[0] // group), 0, 0)),
            pl.BlockSpec((group, rows, width), lambda j, c: (jnp.minimum(j, c[0] // group), 0, part)),
        ],
        out_specs=pl.BlockSpec((rows, width), lambda j, c: (0, 0)),
        scratch_shapes=[
            pltpu.VMEM((heads, rows, HDIM), jnp.float32),
            pltpu.VMEM((heads, rows, HDIM), jnp.float32),
            pltpu.VMEM((heads, rows, HDIM), jnp.float32),
        ],
    )
    return pl.pallas_call(
        kernel,
        grid_spec=grid_spec,
        out_shape=jax.ShapeDtypeStruct((rows, width), jnp.bfloat16),
        compiler_params=pltpu.CompilerParams(dimension_semantics=("arbitrary",)),
    )(jnp.reshape(shard, (1,)).astype(jnp.int32), q_glob, kt_all, v_all)


SWAP = [(0, 1), (1, 0)]


def exchange_heads(x, groups, width):
    if groups != 2:
        split = x.reshape(x.shape[0], groups, width)
        return lax.all_to_all(split, "hg", split_axis=1, concat_axis=0, tiled=True)[:, 0]
    first = lax.axis_index("hg") == 0
    own = jnp.where(first, x[:, :width], x[:, width:])
    got = lax.ppermute(jnp.where(first, x[:, width:], x[:, :width]), "hg", SWAP)
    return jnp.where(
        first, jnp.concatenate([own, got], axis=0), jnp.concatenate([got, own], axis=0)
    )


def project_out(parts, out_weight, w_other, groups):
    if groups != 2:
        return lax.psum_scatter(
            jnp.dot(
                jnp.concatenate(parts, axis=1), out_weight, preferred_element_type=jnp.float32
            ).astype(jnp.bfloat16),
            "hg",
            scatter_dimension=0,
            tiled=True,
        )
    half = parts[0].shape[0] // 2
    first = lax.axis_index("hg") == 0
    got = [
        lax.ppermute(jnp.where(first, a[half:], a[:half]), "hg", SWAP) for a in parts
    ]
    mine = jnp.concatenate([jnp.where(first, a[:half], a[half:]) for a in parts], axis=1)
    total = jnp.dot(mine, out_weight, preferred_element_type=jnp.float32)
    got = jnp.concatenate(got, axis=1)
    cut = w_other[0].shape[0]
    total = total + jnp.dot(got[:, :cut], w_other[0], preferred_element_type=jnp.float32)
    if w_other[1] is not None:
        total = total + jnp.dot(got[:, cut:], w_other[1], preferred_element_type=jnp.float32)
    return total.astype(jnp.bfloat16)


def local(queries, keys, values, reflect_ids, reflect_bank, out_weight):
    groups = lax.axis_size("hg")
    heads = reflect_ids.shape[1]
    width = heads * HDIM
    q_local, k_local, v_local = (exchange_heads(x, groups, width) for x in (queries, keys, values))
    rows = q_local.shape[0]
    v_all = lax.all_gather(v_local, "ctx", axis=0, tiled=False)

    nblocks = rows // BLK
    bank = reflect_bank.shape[0]
    table = reflect_bank.reshape(bank, heads, HDIM).transpose(1, 0, 2)
    onehot = (
        reflect_ids.T[:, :, None] == lax.broadcasted_iota(jnp.int32, (1, 1, bank), 2)
    ).astype(reflect_bank.dtype)
    chosen = jnp.einsum(
        "htb,hbd->htd", onehot, table, preferred_element_type=jnp.float32
    )
    vectors = chosen * lax.rsqrt(jnp.sum(chosen * chosen, axis=-1, keepdims=True) + 1e-06)
    blocks = vectors.reshape(heads, nblocks, BLK, HDIM)
    gram = jnp.einsum("hnkd,hnjd->hnkj", blocks, blocks, precision=HP)
    cut = max(1, (3 * heads) // 8) * HDIM
    w_rest = out_weight[cut:] if groups == 2 and cut < width else None
    gram, q_local, k_local, v_local, w_rest = lax.optimization_barrier(
        (gram, q_local, k_local, v_local, w_rest)
    )
    coupling = 2.0 * jnp.triu(gram, 1)
    tri_factor = 2.0 * invert_unit_upper(coupling)
    spread = jnp.einsum("hnkj,hnje->hnke", tri_factor, blocks, precision=HP)
    eye_d = jnp.eye(HDIM, dtype=jnp.float32)
    block_mats = eye_d - jnp.einsum("hnkd,hnke->hnde", blocks, spread, precision=HP)
    lower_mask = jnp.tril(jnp.ones((BLK, BLK), dtype=jnp.bool_))

    inner_prefix, shard_prod = exclusive_blocks(block_mats)
    parts = 4 if heads % 4 == 0 else (2 if heads % 2 == 0 else 1)
    pw = width // parts
    w_other = [None, None]
    if groups == 2:
        w_other = [lax.ppermute(out_weight[:cut], "hg", SWAP), None]
        if w_rest is not None:
            w_other[1] = lax.ppermute(w_rest, "hg", SWAP)
    earlier_prod, v_all, w_other[0] = lax.optimization_barrier(
        (exclusive_shards(shard_prod, "ctx"), v_all, w_other[0])
    )

    def in_shard(matrix):
        split = matrix.astype(jnp.float32).reshape(nblocks, BLK, heads, HDIM).transpose(2, 0, 1, 3)
        proj = jnp.einsum("hnid,hnkd->hnik", split, blocks, precision=HP)
        proj = jnp.where(lower_mask, proj, 0.0)
        coef = jnp.einsum("hnik,hnrk->hnir", proj, tri_factor, precision=HP)
        inblock = split - jnp.einsum("hnir,hnrd->hnid", coef, blocks, precision=HP)
        moved = jnp.einsum("hnid,hned->hnie", inblock, inner_prefix, precision=HP)
        return moved.reshape(heads, rows, HDIM)

    kt_glob = jnp.einsum(
        "hie,hfe->hfi", in_shard(k_local), earlier_prod, precision=HP
    ).reshape(width, rows).astype(jnp.bfloat16)
    kt_parts = [
        lax.all_gather(kt_glob[p * pw : (p + 1) * pw], "ctx", axis=0, tiled=False)
        for p in range(parts)
    ]
    q_glob = (
        jnp.einsum("hie,hfe->hif", in_shard(q_local), earlier_prod, precision=HP)
        .transpose(1, 0, 2)
        .reshape(rows, width)
        .astype(jnp.bfloat16)
    )
    shard = lax.axis_index("ctx")
    attn = [
        flash_attend(q_glob[:, p * pw : (p + 1) * pw], kt_parts[p], v_all, p, shard, heads // parts)
        for p in range(parts)
    ]
    return project_out(attn, out_weight, w_other, groups)


def solution(mesh):
    placed = (
        P(("ctx", "hg"), None),
        P(("ctx", "hg"), None),
        P(("ctx", "hg"), None),
        P("ctx", "hg"),
        P(None, "hg"),
        P("hg", None),
    )
    return jax.shard_map(
        local, mesh=mesh, in_specs=placed, out_specs=P(("ctx", "hg"), None), check_vma=False
    )
```

```python
import math

import jax
import jax.numpy as jnp
from jax import lax
from jax.experimental import pallas as pl
from jax.experimental.pallas import tpu as pltpu
from jax.sharding import PartitionSpec as P

HDIM = 128
BLK = 32
GROUP = 1
HP = lax.Precision.HIGHEST


def mm(a, b):
    return jnp.einsum("...ij,...jk->...ik", a, b, precision=HP)


def invert_unit_upper(strict):
    eye_blk = jnp.eye(strict.shape[-1], dtype=jnp.float32)
    result = eye_blk - strict
    power = strict
    steps = strict.shape[-1].bit_length()
    for level in range(steps):
        power = mm(power, power)
        result = mm(result, eye_blk + power)
    return result


def exclusive_blocks(mats):
    heads, n, d, _ = mats.shape
    eye = jnp.broadcast_to(jnp.eye(d, dtype=jnp.float32), (heads, 1, d, d))
    acc = jnp.concatenate([eye, mats[:, :-1]], axis=1)
    shift = 1
    while shift < n:
        earlier = jnp.concatenate(
            [jnp.broadcast_to(eye, (heads, shift, d, d)), acc[:, : n - shift]], axis=1
        )
        acc = mm(earlier, acc)
        shift *= 2
    return acc, mm(acc[:, -1], mats[:, -1])


def exclusive_shards(mat, axis):
    length, here = lax.axis_size(axis), lax.axis_index(axis)
    eye = jnp.broadcast_to(jnp.eye(mat.shape[-1], dtype=jnp.float32), mat.shape)
    sizes = []
    rest = length
    for size in (2, 2):
        if rest % size == 0 and rest > size:
            sizes.append(size)
            rest //= size
    sizes.append(rest)
    block, before, stride = mat, eye, 1
    for level, size in enumerate(sizes):
        if size == 1:
            continue
        pos = (here // stride) % size
        last = level == len(sizes) - 1
        if last and size in (3, 4):
            def shifted(x, dist):
                pairs = [
                    (i, i + dist * stride) for i in range(length) if (i // stride) % size + dist < size
                ]
                return jnp.where(pos >= dist, lax.ppermute(x, axis, pairs), eye)

            prev = shifted(block, 1)
            lead = mm(shifted(mm(prev, block), 2), prev)
            before = mm(lead, before)
            break
        got = {}
        for dist in range(1, size):
            forward = [
                (i, i + dist * stride) for i in range(length) if (i // stride) % size + dist < size
            ]
            got[dist] = lax.ppermute(block, axis, forward)
            if not last:
                got[-dist] = lax.ppermute(
                    block, axis, [(b, a) for a, b in forward]
                )
        lead = eye
        for dist in range(size - 1, 0, -1):
            lead = mm(lead, jnp.where(pos >= dist, got[dist], eye))
        before = mm(lead, before)
        if not last:
            tail = block
            for dist in range(1, size):
                tail = mm(tail, jnp.where(pos + dist < size, got[-dist], eye))
            block = mm(lead, tail)
        stride *= size
    return before


def flash_attend(q_glob, kt_all, v_all, part, shard, heads, group=GROUP):
    rows, width = q_glob.shape
    nk = kt_all.shape[0]
    while nk % group:
        group //= 2
    nb = nk // group
    scale = 1.0 / math.sqrt(HDIM)

    def kernel(c_ref, q_ref, k_ref, v_ref, o_ref, m_sc, l_sc, acc_sc):
        j = pl.program_id(0)
        c = c_ref[0]

        @pl.when(j == 0)
        def _():
            m_sc[...] = jnp.full(m_sc.shape, -1e30, jnp.float32)
            l_sc[...] = jnp.zeros(l_sc.shape, jnp.float32)
            acc_sc[...] = jnp.zeros(acc_sc.shape, jnp.float32)

        def step(g, masked):
            for hh in range(heads):
                sl = slice(hh * HDIM, (hh + 1) * HDIM)
                qh = q_ref[:, sl]
                kh = k_ref[g, sl, :]
                vh = v_ref[g, :, sl]
                s = jnp.dot(qh, kh, preferred_element_type=jnp.float32) * scale
                if masked:
                    row = lax.broadcasted_iota(jnp.int32, s.shape, 0)
                    col = lax.broadcasted_iota(jnp.int32, s.shape, 1)
                    allowed = col <= row
                    s = jnp.where(allowed, s, -1e30)
                m_prev = m_sc[hh]
                m_new = jnp.maximum(m_prev, jnp.max(s, axis=1, keepdims=True))
                if s.shape[1] % HDIM == 0:
                    wide = jnp.concatenate([m_new] * (s.shape[1] // HDIM), axis=1)
                else:
                    wide = m_new[:, :1]
                p = jnp.exp(s - wide)
                if masked:
                    p = jnp.where(allowed, p, 0.0)
                fade = jnp.exp(m_prev - m_new)
                l_sc[hh] = l_sc[hh] * fade + jnp.sum(p, axis=1, keepdims=True)
                acc_sc[hh] = acc_sc[hh] * fade + jnp.dot(
                    p.astype(jnp.bfloat16), vh, preferred_element_type=jnp.float32
                )
                m_sc[hh] = m_new

        for g in range(group):
            here = j * group + g

            @pl.when(here < c)
            def _():
                step(g, False)

            @pl.when(here == c)
            def _():
                step(g, True)

        @pl.when(j == nb - 1)
        def _():
            for hh in range(heads):
                sl = slice(hh * HDIM, (hh + 1) * HDIM)
                o_ref[:, sl] = (acc_sc[hh] / l_sc[hh]).astype(o_ref.dtype)

    grid_spec = pltpu.PrefetchScalarGridSpec(
        num_scalar_prefetch=1,
        grid=(nb,),
        in_specs=[
            pl.BlockSpec((rows, width), lambda j, c: (0, 0)),
            pl.BlockSpec((group, width, rows), lambda j, c: (jnp.minimum(j, c[0] // group), 0, 0)),
            pl.BlockSpec((group, rows, width), lambda j, c: (jnp.minimum(j, c[0] // group), 0, part)),
        ],
        out_specs=pl.BlockSpec((rows, width), lambda j, c: (0, 0)),
        scratch_shapes=[
            pltpu.VMEM((heads, rows, HDIM), jnp.float32),
            pltpu.VMEM((heads, rows, HDIM), jnp.float32),
            pltpu.VMEM((heads, rows, HDIM), jnp.float32),
        ],
    )
    return pl.pallas_call(
        kernel,
        grid_spec=grid_spec,
        out_shape=jax.ShapeDtypeStruct((rows, width), jnp.bfloat16),
        compiler_params=pltpu.CompilerParams(dimension_semantics=("arbitrary",)),
    )(jnp.reshape(shard, (1,)).astype(jnp.int32), q_glob, kt_all, v_all)


SWAP = [(0, 1), (1, 0)]


def exchange_heads(x, groups, width):
    if groups != 2:
        split = x.reshape(x.shape[0], groups, width)
        return lax.all_to_all(split, "hg", split_axis=1, concat_axis=0, tiled=True)[:, 0]
    first = lax.axis_index("hg") == 0
    own = jnp.where(first, x[:, :width], x[:, width:])
    got = lax.ppermute(jnp.where(first, x[:, width:], x[:, :width]), "hg", SWAP)
    return jnp.where(
        first, jnp.concatenate([own, got], axis=0), jnp.concatenate([got, own], axis=0)
    )


def project_out(parts, out_weight, w_other, groups):
    if groups != 2:
        return lax.psum_scatter(
            jnp.dot(
                jnp.concatenate(parts, axis=1), out_weight, preferred_element_type=jnp.float32
            ).astype(jnp.bfloat16),
            "hg",
            scatter_dimension=0,
            tiled=True,
        )
    half = parts[0].shape[0] // 2
    first = lax.axis_index("hg") == 0
    got = [
        lax.ppermute(jnp.where(first, a[half:], a[:half]), "hg", SWAP) for a in parts
    ]
    mine = jnp.concatenate([jnp.where(first, a[:half], a[half:]) for a in parts], axis=1)
    total = jnp.dot(mine, out_weight, preferred_element_type=jnp.float32)
    got = jnp.concatenate(got, axis=1)
    cut = w_other[0].shape[0]
    total = total + jnp.dot(got[:, :cut], w_other[0], preferred_element_type=jnp.float32)
    if w_other[1] is not None:
        total = total + jnp.dot(got[:, cut:], w_other[1], preferred_element_type=jnp.float32)
    return total.astype(jnp.bfloat16)


def local(queries, keys, values, reflect_ids, reflect_bank, out_weight):
    groups = lax.axis_size("hg")
    heads = reflect_ids.shape[1]
    width = heads * HDIM
    q_local, k_local, v_local = (exchange_heads(x, groups, width) for x in (queries, keys, values))
    rows = q_local.shape[0]
    v_all = lax.all_gather(v_local, "ctx", axis=0, tiled=False)

    nblocks = rows // BLK
    bank = reflect_bank.shape[0]
    table = reflect_bank.reshape(bank, heads, HDIM).transpose(1, 0, 2)
    onehot = (
        reflect_ids.T[:, :, None] == lax.broadcasted_iota(jnp.int32, (1, 1, bank), 2)
    ).astype(reflect_bank.dtype)
    chosen = jnp.einsum(
        "htb,hbd->htd", onehot, table, preferred_element_type=jnp.float32
    )
    vectors = chosen * lax.rsqrt(jnp.sum(chosen * chosen, axis=-1, keepdims=True) + 1e-06)
    blocks = vectors.reshape(heads, nblocks, BLK, HDIM)
    gram = jnp.einsum("hnkd,hnjd->hnkj", blocks, blocks, precision=HP)
    cut = max(1, (3 * heads) // 8) * HDIM
    w_rest = out_weight[cut:] if groups == 2 and cut < width else None
    gram, q_local, k_local, v_local, w_rest = lax.optimization_barrier(
        (gram, q_local, k_local, v_local, w_rest)
    )
    coupling = 2.0 * jnp.triu(gram, 1)
    tri_factor = 2.0 * invert_unit_upper(coupling)
    spread = jnp.einsum("hnkj,hnje->hnke", tri_factor, blocks, precision=HP)
    eye_d = jnp.eye(HDIM, dtype=jnp.float32)
    block_mats = eye_d - jnp.einsum("hnkd,hnke->hnde", blocks, spread, precision=HP)
    lower_mask = jnp.tril(jnp.ones((BLK, BLK), dtype=jnp.bool_))

    inner_prefix, shard_prod = exclusive_blocks(block_mats)
    parts = 2 if heads % 2 == 0 else 1
    pw = width // parts
    w_other = [None, None]
    if groups == 2:
        w_other = [lax.ppermute(out_weight[:cut], "hg", SWAP), None]
        if w_rest is not None:
            w_other[1] = lax.ppermute(w_rest, "hg", SWAP)
    earlier_prod, v_all, w_other[0] = lax.optimization_barrier(
        (exclusive_shards(shard_prod, "ctx"), v_all, w_other[0])
    )

    def in_shard(matrix):
        split = matrix.astype(jnp.float32).reshape(nblocks, BLK, heads, HDIM).transpose(2, 0, 1, 3)
        proj = jnp.einsum("hnid,hnkd->hnik", split, blocks, precision=HP)
        proj = jnp.where(lower_mask, proj, 0.0)
        coef = jnp.einsum("hnik,hnrk->hnir", proj, tri_factor, precision=HP)
        inblock = split - jnp.einsum("hnir,hnrd->hnid", coef, blocks, precision=HP)
        moved = jnp.einsum("hnid,hned->hnie", inblock, inner_prefix, precision=HP)
        return moved.reshape(heads, rows, HDIM)

    kt_glob = jnp.einsum(
        "hie,hfe->hfi", in_shard(k_local), earlier_prod, precision=HP
    ).reshape(width, rows).astype(jnp.bfloat16)
    kt_parts = [
        lax.all_gather(kt_glob[p * pw : (p + 1) * pw], "ctx", axis=0, tiled=False)
        for p in range(parts)
    ]
    q_glob = (
        jnp.einsum("hie,hfe->hif", in_shard(q_local), earlier_prod, precision=HP)
        .transpose(1, 0, 2)
        .reshape(rows, width)
        .astype(jnp.bfloat16)
    )
    shard = lax.axis_index("ctx")
    attn = [
        flash_attend(q_glob[:, p * pw : (p + 1) * pw], kt_parts[p], v_all, p, shard, heads // parts)
        for p in range(parts)
    ]
    return project_out(attn, out_weight, w_other, groups)


def solution(mesh):
    placed = (
        P(("ctx", "hg"), None),
        P(("ctx", "hg"), None),
        P(("ctx", "hg"), None),
        P("ctx", "hg"),
        P(None, "hg"),
        P("hg", None),
    )
    return jax.shard_map(
        local, mesh=mesh, in_specs=placed, out_specs=P(("ctx", "hg"), None), check_vma=False
    )
```

```python
import math

import jax
import jax.numpy as jnp
from jax import lax
from jax.experimental import pallas as pl
from jax.experimental.pallas import tpu as pltpu
from jax.sharding import PartitionSpec as P

HDIM = 128
BLK = 32
GROUP = 1
HP = lax.Precision.HIGHEST


def mm(a, b):
    return jnp.einsum("...ij,...jk->...ik", a, b, precision=HP)


def invert_unit_upper(strict):
    eye_blk = jnp.eye(strict.shape[-1], dtype=jnp.float32)
    result = eye_blk - strict
    power = strict
    steps = strict.shape[-1].bit_length()
    for level in range(steps):
        power = mm(power, power)
        result = mm(result, eye_blk + power)
    return result


def exclusive_blocks(mats):
    heads, n, d, _ = mats.shape
    eye = jnp.broadcast_to(jnp.eye(d, dtype=jnp.float32), (heads, 1, d, d))
    acc = jnp.concatenate([eye, mats[:, :-1]], axis=1)
    shift = 1
    while shift < n:
        earlier = jnp.concatenate(
            [jnp.broadcast_to(eye, (heads, shift, d, d)), acc[:, : n - shift]], axis=1
        )
        acc = mm(earlier, acc)
        shift *= 2
    return acc, mm(acc[:, -1], mats[:, -1])


def exclusive_shards(mat, axis):
    length, here = lax.axis_size(axis), lax.axis_index(axis)
    eye = jnp.broadcast_to(jnp.eye(mat.shape[-1], dtype=jnp.float32), mat.shape)
    sizes = []
    rest = length
    for size in (2, 2):
        if rest % size == 0 and rest > size:
            sizes.append(size)
            rest //= size
    sizes.append(rest)
    block, before, stride = mat, eye, 1
    for level, size in enumerate(sizes):
        if size == 1:
            continue
        pos = (here // stride) % size
        last = level == len(sizes) - 1
        got = {}
        for dist in range(1, size):
            forward = [
                (i, i + dist * stride) for i in range(length) if (i // stride) % size + dist < size
            ]
            got[dist] = lax.ppermute(block, axis, forward)
            if not last:
                got[-dist] = lax.ppermute(
                    block, axis, [(b, a) for a, b in forward]
                )
        lead = eye
        for dist in range(size - 1, 0, -1):
            lead = mm(lead, jnp.where(pos >= dist, got[dist], eye))
        before = mm(lead, before)
        if not last:
            tail = block
            for dist in range(1, size):
                tail = mm(tail, jnp.where(pos + dist < size, got[-dist], eye))
            block = mm(lead, tail)
        stride *= size
    return before


def flash_attend(q_glob, kt_all, v_all, part, shard, heads, group=GROUP):
    rows, width = q_glob.shape
    nk = kt_all.shape[0]
    while nk % group:
        group //= 2
    nb = nk // group
    scale = 1.0 / math.sqrt(HDIM)

    def kernel(c_ref, q_ref, k_ref, v_ref, o_ref, m_sc, l_sc, acc_sc):
        j = pl.program_id(0)
        c = c_ref[0]

        @pl.when(j == 0)
        def _():
            m_sc[...] = jnp.full(m_sc.shape, -1e30, jnp.float32)
            l_sc[...] = jnp.zeros(l_sc.shape, jnp.float32)
            acc_sc[...] = jnp.zeros(acc_sc.shape, jnp.float32)

        def step(g, masked):
            for hh in range(heads):
                sl = slice(hh * HDIM, (hh + 1) * HDIM)
                qh = q_ref[:, sl]
                kh = k_ref[g, sl, :]
                vh = v_ref[g, :, sl]
                s = jnp.dot(qh, kh, preferred_element_type=jnp.float32)
                if masked:
                    row = lax.broadcasted_iota(jnp.int32, s.shape, 0)
                    col = lax.broadcasted_iota(jnp.int32, s.shape, 1)
                    allowed = col <= row
                    s = jnp.where(allowed, s, -1e30)
                m_prev = m_sc[hh]
                m_new = jnp.maximum(m_prev, jnp.max(s, axis=1, keepdims=True))
                if s.shape[1] % HDIM == 0:
                    wide = jnp.concatenate([m_new] * (s.shape[1] // HDIM), axis=1)
                else:
                    wide = m_new[:, :1]
                p = jnp.exp((s - wide) * scale)
                if masked:
                    p = jnp.where(allowed, p, 0.0)
                fade = jnp.exp((m_prev - m_new) * scale)
                l_sc[hh] = l_sc[hh] * fade + jnp.sum(p, axis=1, keepdims=True)
                acc_sc[hh] = acc_sc[hh] * fade + jnp.dot(
                    p.astype(jnp.bfloat16), vh, preferred_element_type=jnp.float32
                )
                m_sc[hh] = m_new

        for g in range(group):
            here = j * group + g

            @pl.when(here < c)
            def _():
                step(g, False)

            @pl.when(here == c)
            def _():
                step(g, True)

        @pl.when(j == nb - 1)
        def _():
            for hh in range(heads):
                sl = slice(hh * HDIM, (hh + 1) * HDIM)
                o_ref[:, sl] = (acc_sc[hh] / l_sc[hh]).astype(o_ref.dtype)

    grid_spec = pltpu.PrefetchScalarGridSpec(
        num_scalar_prefetch=1,
        grid=(nb,),
        in_specs=[
            pl.BlockSpec((rows, width), lambda j, c: (0, 0)),
            pl.BlockSpec((group, width, rows), lambda j, c: (jnp.minimum(j, c[0] // group), 0, 0)),
            pl.BlockSpec((group, rows, width), lambda j, c: (jnp.minimum(j, c[0] // group), 0, part)),
        ],
        out_specs=pl.BlockSpec((rows, width), lambda j, c: (0, 0)),
        scratch_shapes=[
            pltpu.VMEM((heads, rows, HDIM), jnp.float32),
            pltpu.VMEM((heads, rows, HDIM), jnp.float32),
            pltpu.VMEM((heads, rows, HDIM), jnp.float32),
        ],
    )
    return pl.pallas_call(
        kernel,
        grid_spec=grid_spec,
        out_shape=jax.ShapeDtypeStruct((rows, width), jnp.bfloat16),
        compiler_params=pltpu.CompilerParams(dimension_semantics=("arbitrary",)),
    )(jnp.reshape(shard, (1,)).astype(jnp.int32), q_glob, kt_all, v_all)


SWAP = [(0, 1), (1, 0)]


def exchange_heads(x, groups, width):
    if groups != 2:
        split = x.reshape(x.shape[0], groups, width)
        return lax.all_to_all(split, "hg", split_axis=1, concat_axis=0, tiled=True)[:, 0]
    first = lax.axis_index("hg") == 0
    own = jnp.where(first, x[:, :width], x[:, width:])
    got = lax.ppermute(jnp.where(first, x[:, width:], x[:, :width]), "hg", SWAP)
    return jnp.where(
        first, jnp.concatenate([own, got], axis=0), jnp.concatenate([got, own], axis=0)
    )


def project_out(parts, out_weight, w_other, groups):
    if groups != 2:
        return lax.psum_scatter(
            jnp.dot(
                jnp.concatenate(parts, axis=1), out_weight, preferred_element_type=jnp.float32
            ).astype(jnp.bfloat16),
            "hg",
            scatter_dimension=0,
            tiled=True,
        )
    half = parts[0].shape[0] // 2
    first = lax.axis_index("hg") == 0
    got = [
        lax.ppermute(jnp.where(first, a[half:], a[:half]), "hg", SWAP) for a in parts
    ]
    mine = jnp.concatenate([jnp.where(first, a[:half], a[half:]) for a in parts], axis=1)
    total = jnp.dot(mine, out_weight, preferred_element_type=jnp.float32)
    got = jnp.concatenate(got, axis=1)
    cut = w_other[0].shape[0]
    total = total + jnp.dot(got[:, :cut], w_other[0], preferred_element_type=jnp.float32)
    if w_other[1] is not None:
        total = total + jnp.dot(got[:, cut:], w_other[1], preferred_element_type=jnp.float32)
    return total.astype(jnp.bfloat16)


def local(queries, keys, values, reflect_ids, reflect_bank, out_weight):
    groups = lax.axis_size("hg")
    heads = reflect_ids.shape[1]
    width = heads * HDIM
    q_local, k_local, v_local = (exchange_heads(x, groups, width) for x in (queries, keys, values))
    rows = q_local.shape[0]
    v_all = lax.all_gather(v_local, "ctx", axis=0, tiled=False)

    nblocks = rows // BLK
    bank = reflect_bank.shape[0]
    table = reflect_bank.reshape(bank, heads, HDIM).transpose(1, 0, 2)
    onehot = (
        reflect_ids.T[:, :, None] == lax.broadcasted_iota(jnp.int32, (1, 1, bank), 2)
    ).astype(reflect_bank.dtype)
    chosen = jnp.einsum(
        "htb,hbd->htd", onehot, table, preferred_element_type=jnp.float32
    )
    vectors = chosen * lax.rsqrt(jnp.sum(chosen * chosen, axis=-1, keepdims=True) + 1e-06)
    blocks = vectors.reshape(heads, nblocks, BLK, HDIM)
    gram = jnp.einsum("hnkd,hnjd->hnkj", blocks, blocks, precision=HP)
    cut = max(1, (3 * heads) // 8) * HDIM
    w_rest = out_weight[cut:] if groups == 2 and cut < width else None
    gram, q_local, k_local, v_local, w_rest = lax.optimization_barrier(
        (gram, q_local, k_local, v_local, w_rest)
    )
    coupling = 2.0 * jnp.triu(gram, 1)
    tri_factor = 2.0 * invert_unit_upper(coupling)
    spread = jnp.einsum("hnkj,hnje->hnke", tri_factor, blocks, precision=HP)
    eye_d = jnp.eye(HDIM, dtype=jnp.float32)
    block_mats = eye_d - jnp.einsum("hnkd,hnke->hnde", blocks, spread, precision=HP)
    lower_mask = jnp.tril(jnp.ones((BLK, BLK), dtype=jnp.bool_))

    inner_prefix, shard_prod = exclusive_blocks(block_mats)
    parts = 2 if heads % 2 == 0 else 1
    pw = width // parts
    w_other = [None, None]
    if groups == 2:
        w_other = [lax.ppermute(out_weight[:cut], "hg", SWAP), None]
        if w_rest is not None:
            w_other[1] = lax.ppermute(w_rest, "hg", SWAP)
    earlier_prod, v_all, w_other[0] = lax.optimization_barrier(
        (exclusive_shards(shard_prod, "ctx"), v_all, w_other[0])
    )

    def in_shard(matrix):
        split = matrix.astype(jnp.float32).reshape(nblocks, BLK, heads, HDIM).transpose(2, 0, 1, 3)
        proj = jnp.einsum("hnid,hnkd->hnik", split, blocks, precision=HP)
        proj = jnp.where(lower_mask, proj, 0.0)
        coef = jnp.einsum("hnik,hnrk->hnir", proj, tri_factor, precision=HP)
        inblock = split - jnp.einsum("hnir,hnrd->hnid", coef, blocks, precision=HP)
        moved = jnp.einsum("hnid,hned->hnie", inblock, inner_prefix, precision=HP)
        return moved.reshape(heads, rows, HDIM)

    kt_glob = jnp.einsum(
        "hie,hfe->hfi", in_shard(k_local), earlier_prod, precision=HP
    ).reshape(width, rows).astype(jnp.bfloat16)
    kt_parts = [
        lax.all_gather(kt_glob[p * pw : (p + 1) * pw], "ctx", axis=0, tiled=False)
        for p in range(parts)
    ]
    q_glob = (
        jnp.einsum("hie,hfe->hif", in_shard(q_local), earlier_prod, precision=HP)
        .transpose(1, 0, 2)
        .reshape(rows, width)
        .astype(jnp.bfloat16)
    )
    shard = lax.axis_index("ctx")
    attn = [
        flash_attend(q_glob[:, p * pw : (p + 1) * pw], kt_parts[p], v_all, p, shard, heads // parts)
        for p in range(parts)
    ]
    return project_out(attn, out_weight, w_other, groups)


def solution(mesh):
    placed = (
        P(("ctx", "hg"), None),
        P(("ctx", "hg"), None),
        P(("ctx", "hg"), None),
        P("ctx", "hg"),
        P(None, "hg"),
        P("hg", None),
    )
    return jax.shard_map(
        local, mesh=mesh, in_specs=placed, out_specs=P(("ctx", "hg"), None), check_vma=False
    )
```
